32 devices in a mesh: blk: 8 (over y, x, core), head: 4 (over z).
Axes of the slice: x: 2, y: 2, z: 4, core: 2. Of those that a mesh axis runs over, the one named last changes fastest.
Arguments:
- query_matrix: bfloat16 [4096, 4096], P(('blk', 'head')), may hold values from -6 to 6
- key_matrix: bfloat16 [4096, 512], P(('blk', 'head')), may hold values from -6 to 6
- value_matrix: bfloat16 [4096, 512], P(('blk', 'head')), may hold values from -6 to 6
- output_cotangent: bfloat16 [4096, 4096], P(('blk', 'head')), may hold values from -6 to 6
- forward_output: bfloat16 [4096, 4096], P(('blk', 'head')), may hold values from -6 to 6
- doc_ids: int32 [4096], P(('blk', 'head')), may hold values from 0 to 31, never falling along the last dimension, each value on 1 to 2048 neighbouring positions
Outputs:
- query_grad: bfloat16 [4096, 4096], P(('blk', 'head'))
- key_gradient: bfloat16 [4096, 512], P(('blk', 'head'))
- value_gradient: bfloat16 [4096, 512], P(('blk', 'head'))
The draws below stay inside these ranges and needn't reach their ends.
Inputs may be any that keep to these rules, and one draw needn't show every extreme that they name: `doc_ids`: document numbers never fall along the window; every document has 2048 tokens or fewer and one has exactly 2048.
All inputs are finite; a program needn't handle non-finite values.
Results may differ from the reference program's by a relative error of at most 0.0051.
Values may be sent and summed in bfloat16 or wider, within the bound.
No kernel may reach another device: no remote copies, remote signals or barrier semaphores. Data moves between devices by JAX's collectives and lax.ppermute only.
A program may use at most 64 MiB of HBM per device.

```python
import math
import jax
import jax.numpy as jnp
import numpy as np
from jax import lax

QUERY_HEAD_COUNT = 32
KEY_VALUE_HEADS = 4
HEAD_WIDTH = 128
BLK = 512
WINDOW_TOKENS = 4096
DOCS = 32
LONGEST_DOCUMENT = 2048
N_BLK = 8


def draw_query_matrix(key, part):
    value_tensor = jnp.clip(jax.random.normal(jax.random.fold_in(key, 1), (WINDOW_TOKENS, KEY_VALUE_HEADS, QUERY_HEAD_COUNT // KEY_VALUE_HEADS, HEAD_WIDTH), jnp.float32), -6.0, 6.0)
    return value_tensor.reshape(WINDOW_TOKENS, QUERY_HEAD_COUNT * HEAD_WIDTH).astype(jnp.bfloat16)


def draw_key_matrix(key, part):
    value_tensor = jnp.clip(jax.random.normal(jax.random.fold_in(key, 2), (WINDOW_TOKENS, KEY_VALUE_HEADS, HEAD_WIDTH), jnp.float32), -6.0, 6.0)
    return value_tensor.reshape(WINDOW_TOKENS, KEY_VALUE_HEADS * HEAD_WIDTH).astype(jnp.bfloat16)


def shard_levels(key, extent, shards, low, high):
    loudness, own = 1.0, jax.random.fold_in(key, 6)
    for dim, parts in shards:
        heights = jnp.exp(jax.random.uniform(jax.random.fold_in(own, dim), (parts,), jnp.float32, low / len(shards), high / len(shards)))
        loudness = loudness * jnp.repeat(heights, extent[dim] // parts).reshape([-1 if axis == dim else 1 for axis in range(len(extent))])
    return loudness


def profile(amount, total, limit, slope):
    weights = [(1 << 20) // math.isqrt(grade ** slope) + 1 for grade in range(2, amount + 1)]
    surplus, counts = total - limit - (amount - 1), [1] * (amount - 1)
    while surplus > 0:
        free = [i for i in range(amount - 1) if counts[i] < limit]
        mass, remaining = sum([weights[i] for i in free]), surplus
        for i in free:
            more = min(limit - counts[i], max(1, remaining * weights[i] // mass), surplus)
            counts[i] = counts[i] + more
            surplus = surplus - more
    return np.array([limit] + counts)


def uneven_parts(stream_key, number_of, total, most, skew):
    if number_of == 2:
        one = jax.random.randint(stream_key, (), max(1, total - most), min(most, total - 1) + 1)
        return jnp.stack([one, total - one])
    sizes = jnp.asarray(profile(number_of, total, most, skew), jnp.int32)
    pairs = (number_of - 1) // 2
    donor, sink = sizes[1:1 + 2 * pairs:2], sizes[2:2 + 2 * pairs:2]
    slack = jnp.minimum(donor - 1, most - sink)
    moved = jax.random.randint(jax.random.fold_in(stream_key, 1), (pairs,), 0, 1 << 20) % (slack + 1)
    sizes = sizes.at[1:1 + 2 * pairs:2].set(donor - moved).at[2:2 + 2 * pairs:2].set(sink + moved)
    return sizes[jax.random.permutation(jax.random.fold_in(stream_key, 2), number_of)]


def gaussian(key, dims, deviation, most, shards=(), held_as=jnp.bfloat16):
    result = jax.random.normal(key, dims, jnp.float32) * deviation
    if len(shards) > 0:
        result = shard_levels(key, dims, shards, -0.22, 0.18) * result
    return jnp.clip(result, min=-most, max=most).astype(held_as)


def setup_inputs(seed: int = 0) -> dict:
    seeds = jax.random.split(jax.random.key(seed), 7)
    return {
        "query_matrix": draw_query_matrix(jax.random.fold_in(seeds[6], 71), 0),
        "key_matrix": draw_key_matrix(jax.random.fold_in(seeds[6], 71), 0),
        "value_matrix": gaussian(seeds[2], (WINDOW_TOKENS, KEY_VALUE_HEADS * HEAD_WIDTH), 1.0, 6.0, ((0, 32),)),
        "output_cotangent": gaussian(seeds[3], (WINDOW_TOKENS, QUERY_HEAD_COUNT * HEAD_WIDTH), 1.0, 6.0, ((0, 32),)),
        "forward_output": gaussian(seeds[4], (WINDOW_TOKENS, QUERY_HEAD_COUNT * HEAD_WIDTH), 1.0, 6.0, ((0, 32),)),
        "doc_ids": jnp.searchsorted(jnp.cumsum(uneven_parts(seeds[5], DOCS, WINDOW_TOKENS, LONGEST_DOCUMENT, 2)), jnp.arange(WINDOW_TOKENS), side="right").astype(jnp.int32),
    }


masked_score = -1e30


def reference(query_matrix, key_matrix, value_matrix, output_cotangent, forward_output, doc_ids):
    heads_per_group = QUERY_HEAD_COUNT // KEY_VALUE_HEADS
    logit_scale = HEAD_WIDTH ** -0.5
    query_tensor = query_matrix.reshape(WINDOW_TOKENS, KEY_VALUE_HEADS, heads_per_group, HEAD_WIDTH)
    returned_grads = output_cotangent.reshape(WINDOW_TOKENS, KEY_VALUE_HEADS, heads_per_group, HEAD_WIDTH)
    stored_output = forward_output.reshape(WINDOW_TOKENS, KEY_VALUE_HEADS, heads_per_group, HEAD_WIDTH)
    row_terms = jnp.sum(returned_grads.astype(jnp.float32) * stored_output.astype(jnp.float32), axis=-1)
    padded_keys = jnp.concatenate([jnp.zeros((LONGEST_DOCUMENT, KEY_VALUE_HEADS, HEAD_WIDTH), jnp.bfloat16), key_matrix.reshape(WINDOW_TOKENS, KEY_VALUE_HEADS, HEAD_WIDTH)], 0)
    padded_values = jnp.concatenate([jnp.zeros((LONGEST_DOCUMENT, KEY_VALUE_HEADS, HEAD_WIDTH), jnp.bfloat16), value_matrix.reshape(WINDOW_TOKENS, KEY_VALUE_HEADS, HEAD_WIDTH)], 0)
    segments_pad = jnp.concatenate([jnp.full((LONGEST_DOCUMENT,), -1, jnp.int32), doc_ids.astype(jnp.int32)], 0)
    window = LONGEST_DOCUMENT + BLK

    def one_block(running, which_block):
        summed_key_grad, summed_value_grad = running
        first_row = (which_block * BLK).astype(jnp.int32)
        query_block = lax.dynamic_slice_in_dim(query_tensor, first_row, BLK, 0).astype(jnp.float32)
        grad_block = lax.dynamic_slice_in_dim(returned_grads, first_row, BLK, 0).astype(jnp.float32)
        terms_block = lax.dynamic_slice_in_dim(row_terms, first_row, BLK, 0).transpose(1, 2, 0)[..., None]
        key_window = lax.dynamic_slice_in_dim(padded_keys, first_row, window, 0).astype(jnp.float32)
        value_window = lax.dynamic_slice_in_dim(padded_values, first_row, window, 0).astype(jnp.float32)
        query_segment = lax.dynamic_slice_in_dim(doc_ids.astype(jnp.int32), first_row, BLK, 0)
        key_segment = lax.dynamic_slice_in_dim(segments_pad, first_row, window, 0)
        query_position = first_row + jnp.arange(BLK, dtype=jnp.int32)
        key_position = first_row - LONGEST_DOCUMENT + jnp.arange(window, dtype=jnp.int32)
        allowed = (query_segment[:, None] == key_segment[None, :]) & (key_position[None, :] <= query_position[:, None])
        scores = jnp.einsum('ighd,jgd->ghij', query_block, key_window) * logit_scale
        scores = jnp.where(allowed, scores, masked_score)
        row_max = jnp.max(scores, axis=-1, keepdims=True)
        log_total = row_max + jnp.log(jnp.sum(jnp.where(allowed, jnp.exp(scores - row_max), 0.0), axis=-1, keepdims=True))
        probabilities = jnp.where(allowed, jnp.exp(scores - log_total), 0.0)
        weights_half = lax.optimization_barrier(probabilities.astype(jnp.bfloat16)).astype(jnp.float32)
        prob_grad = jnp.einsum('ighd,jgd->ghij', grad_block, value_window)
        score_grad = lax.optimization_barrier((probabilities * (prob_grad - terms_block)).astype(jnp.bfloat16)).astype(jnp.float32)
        value_part = jnp.einsum('ghij,ighd->jgd', weights_half, grad_block)
        key_part = jnp.einsum('ghij,ighd->jgd', score_grad, query_block)
        query_part = jnp.einsum('ghij,jgd->ighd', score_grad, key_window)
        summed_key_grad = lax.dynamic_update_slice_in_dim(summed_key_grad, lax.dynamic_slice_in_dim(summed_key_grad, first_row, window, 0) + key_part, first_row, 0)
        summed_value_grad = lax.dynamic_update_slice_in_dim(summed_value_grad, lax.dynamic_slice_in_dim(summed_value_grad, first_row, window, 0) + value_part, first_row, 0)
        return (summed_key_grad, summed_value_grad), query_part

    starting_state = (jnp.zeros((WINDOW_TOKENS + LONGEST_DOCUMENT, KEY_VALUE_HEADS, HEAD_WIDTH), jnp.float32), jnp.zeros((WINDOW_TOKENS + LONGEST_DOCUMENT, KEY_VALUE_HEADS, HEAD_WIDTH), jnp.float32))
    (summed_key_grad, summed_value_grad), query_parts = lax.scan(one_block, starting_state, jnp.arange(N_BLK, dtype=jnp.int32))
    query_grad = (query_parts.reshape(WINDOW_TOKENS, QUERY_HEAD_COUNT * HEAD_WIDTH) * logit_scale).astype(jnp.bfloat16)
    key_gradient = (summed_key_grad[LONGEST_DOCUMENT:].reshape(WINDOW_TOKENS, KEY_VALUE_HEADS * HEAD_WIDTH) * logit_scale).astype(jnp.bfloat16)
    value_gradient = summed_value_grad[LONGEST_DOCUMENT:].reshape(WINDOW_TOKENS, KEY_VALUE_HEADS * HEAD_WIDTH).astype(jnp.bfloat16)
    return query_grad, key_gradient, value_gradient
```

```python
import jax
import jax.numpy as jnp
from jax import lax
from jax.sharding import PartitionSpec as P

HEAD_WIDTH = 128
DOC_SPAN = 4


masked_score = -1e30


def shifted(block, axis, distance):
    devices = range(lax.axis_size(axis))
    route = [(i - distance, i) for i in devices if i - distance in devices]
    return lax.ppermute(block, axis, route)


def per_device(query_matrix, key_matrix, value_matrix, output_cotangent, forward_output, doc_ids):
    cycle_size = lax.axis_size("blk")
    head_ways = lax.axis_size("head")
    shard_rows = query_matrix.shape[0]
    block_rows = shard_rows * head_ways
    query_heads = query_matrix.shape[1] // (HEAD_WIDTH * head_ways)
    kv_heads = key_matrix.shape[1] // (HEAD_WIDTH * head_ways)
    heads_per_group = query_heads // kv_heads
    q_cols = query_heads * HEAD_WIDTH
    kv_cols = kv_heads * HEAD_WIDTH
    logit_scale = HEAD_WIDTH ** (-0.5)
    all_heads = query_matrix.shape[1] // HEAD_WIDTH

    row_terms_local = jnp.sum(
        output_cotangent.astype(jnp.float32).reshape(shard_rows, all_heads, HEAD_WIDTH)
        * forward_output.astype(jnp.float32).reshape(shard_rows, all_heads, HEAD_WIDTH),
        axis=-1,
    ).reshape(shard_rows, head_ways, query_heads)
    doc_half = jnp.broadcast_to(
        doc_ids.astype(jnp.bfloat16)[:, None, None], (shard_rows, head_ways, HEAD_WIDTH)
    )
    packed = jnp.concatenate(
        [
            query_matrix.reshape(shard_rows, head_ways, q_cols),
            output_cotangent.reshape(shard_rows, head_ways, q_cols),
            key_matrix.reshape(shard_rows, head_ways, kv_cols),
            value_matrix.reshape(shard_rows, head_ways, kv_cols),
            doc_half,
        ],
        axis=2,
    )
    packed = lax.all_to_all(packed, "head", split_axis=1, concat_axis=0, tiled=True)
    packed = packed.reshape(block_rows, 2 * q_cols + 2 * kv_cols + HEAD_WIDTH)
    row_terms_blk = lax.all_to_all(
        row_terms_local, "head", split_axis=1, concat_axis=0, tiled=True
    ).reshape(block_rows, query_heads)

    query_tensor = packed[:, :q_cols].reshape(block_rows, kv_heads, heads_per_group, HEAD_WIDTH)
    returned_grads = packed[:, q_cols : 2 * q_cols].reshape(
        block_rows, kv_heads, heads_per_group, HEAD_WIDTH
    )
    kvd_local = packed[:, 2 * q_cols :]
    row_terms = row_terms_blk.reshape(block_rows, kv_heads, heads_per_group).transpose(1, 2, 0)[
        ..., None
    ]

    my_block = lax.axis_index("blk")
    query_segment = kvd_local[:, 2 * kv_cols].astype(jnp.int32)
    query_position = my_block * block_rows + jnp.arange(block_rows, dtype=jnp.int32)
    first_segment = query_segment[0]

    span = min(DOC_SPAN, cycle_size - 1)
    near_blocks = [(kvd_local, 0)]
    for distance in range(1, span + 1):
        near_blocks.append((shifted(kvd_local, "blk", distance), distance))

    def unpack(kvd):
        key_split = kvd[:, :kv_cols].reshape(block_rows, kv_heads, HEAD_WIDTH)
        value_split = kvd[:, kv_cols : 2 * kv_cols].reshape(block_rows, kv_heads, HEAD_WIDTH)
        key_segment = kvd[:, 2 * kv_cols].astype(jnp.int32)
        return key_split, value_split, key_segment

    def shares_doc(kvd, distance):
        if distance == 0:
            return jnp.bool_(True)
        last_segment = kvd[block_rows - 1, 2 * kv_cols].astype(jnp.int32)
        return (my_block - distance >= 0) & (last_segment == first_segment)

    def block_scores(kvd, distance):
        key_split, _, key_segment = unpack(kvd)
        key_position = (my_block - distance) * block_rows + jnp.arange(block_rows, dtype=jnp.int32)
        allowed = (query_segment[:, None] == key_segment[None, :]) & (
            key_position[None, :] <= query_position[:, None]
        )
        scores = (
            jnp.einsum(
                "ighd,jgd->ghij", query_tensor, key_split, preferred_element_type=jnp.float32
            )
            * logit_scale
        )
        return (jnp.where(allowed, scores, masked_score), allowed)

    def add_stats(running, kvd, distance):
        run_max, run_sum = running
        scores, allowed = block_scores(kvd, distance)
        new_max = jnp.maximum(run_max, jnp.max(scores, axis=-1, keepdims=True))
        new_sum = run_sum * jnp.exp(run_max - new_max) + jnp.sum(
            jnp.where(allowed, jnp.exp(scores - new_max), 0.0), axis=-1, keepdims=True
        )
        return (new_max, new_sum)

    start_max = jnp.full((kv_heads, heads_per_group, block_rows, 1), masked_score, jnp.float32)
    start_sum = jnp.zeros((kv_heads, heads_per_group, block_rows, 1), jnp.float32)
    running = (start_max, start_sum)
    for kvd, distance in near_blocks:
        if distance == 0:
            running = add_stats(running, kvd, distance)
        else:
            running = lax.cond(
                shares_doc(kvd, distance),
                lambda inner, kb=kvd, dd=distance: add_stats(inner, kb, dd),
                lambda inner: inner,
                running,
            )
    run_max, run_sum = running
    log_total = run_max + jnp.log(run_sum)

    def block_grads(kvd, distance):
        scores, allowed = block_scores(kvd, distance)
        key_split, value_split, _ = unpack(kvd)
        probabilities = jnp.where(allowed, jnp.exp(scores - log_total), 0.0)
        prob_grad = jnp.einsum(
            "ighd,jgd->ghij", returned_grads, value_split, preferred_element_type=jnp.float32
        )
        score_grad = (probabilities * (prob_grad - row_terms)).astype(jnp.bfloat16)
        weights_half = probabilities.astype(jnp.bfloat16)
        value_part = jnp.einsum(
            "ghij,ighd->jgd", weights_half, returned_grads, preferred_element_type=jnp.float32
        )
        key_part = jnp.einsum(
            "ghij,ighd->jgd", score_grad, query_tensor, preferred_element_type=jnp.float32
        )
        query_part = jnp.einsum(
            "ghij,jgd->ighd", score_grad, key_split, preferred_element_type=jnp.float32
        )
        return (
            query_part.reshape(block_rows, q_cols),
            jnp.concatenate(
                [key_part.reshape(block_rows, kv_cols), value_part.reshape(block_rows, kv_cols)],
                axis=1,
            ),
        )

    def empty_grads():
        return (
            jnp.zeros((block_rows, q_cols), jnp.float32),
            jnp.zeros((block_rows, 2 * kv_cols), jnp.float32),
        )

    query_total, own_kv_grad = block_grads(kvd_local, 0)
    returned = []
    for kvd, distance in near_blocks[1:]:
        query_part, kv_part = lax.cond(
            shares_doc(kvd, distance),
            lambda kb=kvd, dd=distance: block_grads(kb, dd),
            empty_grads,
        )
        query_total = query_total + query_part
        returned.append(shifted(kv_part, "blk", -distance))
    kv_grad = own_kv_grad
    for part in returned:
        kv_grad = kv_grad + part

    query_grad = (query_total * logit_scale).astype(jnp.bfloat16)
    key_gradient = (kv_grad[:, :kv_cols] * logit_scale).astype(jnp.bfloat16)
    value_gradient = kv_grad[:, kv_cols:].astype(jnp.bfloat16)
    out_packed = jnp.concatenate([query_grad, key_gradient, value_gradient], axis=1).reshape(
        head_ways, shard_rows, 1, q_cols + 2 * kv_cols
    )
    out_packed = lax.all_to_all(out_packed, "head", split_axis=0, concat_axis=2, tiled=True)
    out_packed = out_packed.reshape(shard_rows, head_ways, q_cols + 2 * kv_cols)
    return (
        out_packed[:, :, :q_cols].reshape(shard_rows, head_ways * q_cols),
        out_packed[:, :, q_cols : q_cols + kv_cols].reshape(shard_rows, head_ways * kv_cols),
        out_packed[:, :, q_cols + kv_cols :].reshape(shard_rows, head_ways * kv_cols),
    )


def solution(mesh):
    return jax.shard_map(
        per_device,
        mesh=mesh,
        in_specs=(
            P(("blk", "head"), None),
            P(("blk", "head"), None),
            P(("blk", "head"), None),
            P(("blk", "head"), None),
            P(("blk", "head"), None),
            P(("blk", "head")),
        ),
        out_specs=(P(("blk", "head"), None), P(("blk", "head"), None), P(("blk", "head"), None)),
        check_vma=False,
    )
```

```python
import functools

import jax
import jax.numpy as jnp
from jax import lax
from jax.experimental import pallas as pl
from jax.experimental.pallas import tpu as pltpu
from jax.sharding import PartitionSpec as P

HEAD_WIDTH = 128
DOC_SPAN = 4


masked_score = -1e30


def shifted(block, axis, distance):
    devices = range(lax.axis_size(axis))
    route = [(i - distance, i) for i in devices if i - distance in devices]
    return lax.ppermute(block, axis, route)


def attn_kernel(flags_ref, q_ref, do_ref, rt_ref, qdoc_ref, kdoc_ref, k_ref, v_ref,
                dq_ref, dk_ref, dv_ref, m_ref, l_ref, *, n_near, logit_scale):
    head = pl.program_id(0)
    rows = q_ref.shape[0]

    @pl.when(head == 0)
    def _():
        dk_ref[...] = jnp.zeros_like(dk_ref)
        dv_ref[...] = jnp.zeros_like(dv_ref)

    q = q_ref[...]
    do = do_ref[...]
    qdoc = qdoc_ref[...]
    row_id = lax.broadcasted_iota(jnp.int32, (rows, rows), 0)
    col_id = lax.broadcasted_iota(jnp.int32, (rows, rows), 1)

    def allowed_of(d):
        same = qdoc == kdoc_ref[d]
        if d == 0:
            same = same & (col_id <= row_id)
        return same

    def scores_of(d):
        s = lax.dot_general(q, k_ref[d], (((1,), (1,)), ((), ())),
                            preferred_element_type=jnp.float32) * logit_scale
        return s

    m_ref[...] = jnp.full(m_ref.shape, masked_score, jnp.float32)
    l_ref[...] = jnp.zeros(l_ref.shape, jnp.float32)
    for d in range(n_near):
        @pl.when(flags_ref[d] > 0)
        def _():
            allowed = allowed_of(d)
            s = jnp.where(allowed, scores_of(d), masked_score)
            m_old = m_ref[...]
            m_new = jnp.maximum(m_old, jnp.max(s, axis=-1, keepdims=True))
            l_ref[...] = l_ref[...] * jnp.exp(m_old - m_new) + jnp.sum(
                jnp.where(allowed, jnp.exp(s - m_new), 0.0), axis=-1, keepdims=True)
            m_ref[...] = m_new

    log_total = m_ref[...] + jnp.log(l_ref[...])
    rt = rt_ref[0]
    dq_ref[...] = jnp.zeros_like(dq_ref)
    for d in range(n_near):
        @pl.when(flags_ref[d] > 0)
        def _():
            allowed = allowed_of(d)
            s = scores_of(d)
            p = jnp.where(allowed, jnp.exp(s - log_total), 0.0)
            dp = lax.dot_general(do, v_ref[d], (((1,), (1,)), ((), ())),
                                 preferred_element_type=jnp.float32)
            ds = (p * (dp - rt)).astype(jnp.bfloat16)
            pb = p.astype(jnp.bfloat16)
            dv_ref[d] += lax.dot_general(pb, do, (((0,), (0,)), ((), ())),
                                         preferred_element_type=jnp.float32)
            dk_ref[d] += lax.dot_general(ds, q, (((0,), (0,)), ((), ())),
                                         preferred_element_type=jnp.float32)
            dq_ref[...] += jnp.dot(ds, k_ref[d], preferred_element_type=jnp.float32)


def block_attention(flags, q, do, rt, qdoc, kdoc, k, v):
    rows, cols = q.shape
    heads = cols // HEAD_WIDTH
    n_near = k.shape[0]
    kern = functools.partial(attn_kernel, n_near=n_near, logit_scale=HEAD_WIDTH ** (-0.5))
    full3 = lambda shape: pl.BlockSpec(shape, lambda h, f: (0, 0, 0))
    flops = 2 * heads * n_near * rows * rows * HEAD_WIDTH * 6
    return pl.pallas_call(
        kern,
        out_shape=(
            jax.ShapeDtypeStruct((rows, cols), jnp.float32),
            jax.ShapeDtypeStruct((n_near, rows, HEAD_WIDTH), jnp.float32),
            jax.ShapeDtypeStruct((n_near, rows, HEAD_WIDTH), jnp.float32),
        ),
        grid_spec=pltpu.PrefetchScalarGridSpec(
            num_scalar_prefetch=1,
            grid=(heads,),
            in_specs=[
                pl.BlockSpec((rows, HEAD_WIDTH), lambda h, f: (0, h)),
                pl.BlockSpec((rows, HEAD_WIDTH), lambda h, f: (0, h)),
                pl.BlockSpec((1, rows, 1), lambda h, f: (h, 0, 0)),
                pl.BlockSpec((rows, 1), lambda h, f: (0, 0)),
                full3((n_near, 1, rows)),
                full3((n_near, rows, HEAD_WIDTH)),
                full3((n_near, rows, HEAD_WIDTH)),
            ],
            out_specs=[
                pl.BlockSpec((rows, HEAD_WIDTH), lambda h, f: (0, h)),
                full3((n_near, rows, HEAD_WIDTH)),
                full3((n_near, rows, HEAD_WIDTH)),
            ],
            scratch_shapes=[pltpu.VMEM((rows, 1), jnp.float32), pltpu.VMEM((rows, 1), jnp.float32)],
        ),
        compiler_params=pltpu.CompilerParams(dimension_semantics=("arbitrary",)),
        cost_estimate=pl.CostEstimate(flops=flops, transcendentals=2 * heads * n_near * rows * rows,
                                      bytes_accessed=4 * rows * cols * 2 + 8 * n_near * rows * HEAD_WIDTH * 2),
    )(flags, q, do, rt, qdoc, kdoc, k, v)


def per_device(query_matrix, key_matrix, value_matrix, output_cotangent, forward_output, doc_ids):
    cycle_size = lax.axis_size("blk")
    head_ways = lax.axis_size("head")
    shard_rows = query_matrix.shape[0]
    block_rows = shard_rows * head_ways
    query_heads = query_matrix.shape[1] // (HEAD_WIDTH * head_ways)
    kv_heads = key_matrix.shape[1] // (HEAD_WIDTH * head_ways)
    heads_per_group = query_heads // kv_heads
    q_cols = query_heads * HEAD_WIDTH
    kv_cols = kv_heads * HEAD_WIDTH
    logit_scale = HEAD_WIDTH ** (-0.5)
    all_heads = query_matrix.shape[1] // HEAD_WIDTH

    row_terms_local = jnp.sum(
        output_cotangent.astype(jnp.float32).reshape(shard_rows, all_heads, HEAD_WIDTH)
        * forward_output.astype(jnp.float32).reshape(shard_rows, all_heads, HEAD_WIDTH),
        axis=-1,
    ).reshape(shard_rows, head_ways, query_heads)
    doc_half = jnp.broadcast_to(
        doc_ids.astype(jnp.bfloat16)[:, None, None], (shard_rows, head_ways, HEAD_WIDTH)
    )
    packed = jnp.concatenate(
        [
            query_matrix.reshape(shard_rows, head_ways, q_cols),
            output_cotangent.reshape(shard_rows, head_ways, q_cols),
            key_matrix.reshape(shard_rows, head_ways, kv_cols),
            value_matrix.reshape(shard_rows, head_ways, kv_cols),
            doc_half,
        ],
        axis=2,
    )
    packed = lax.all_to_all(packed, "head", split_axis=1, concat_axis=0, tiled=True)
    packed = packed.reshape(block_rows, 2 * q_cols + 2 * kv_cols + HEAD_WIDTH)
    row_terms_blk = lax.all_to_all(
        row_terms_local, "head", split_axis=1, concat_axis=0, tiled=True
    ).reshape(block_rows, query_heads)

    kvd_local = packed[:, 2 * q_cols :]

    my_block = lax.axis_index("blk")
    query_segment = kvd_local[:, 2 * kv_cols].astype(jnp.float32)
    first_segment = query_segment[0]

    span = min(DOC_SPAN, cycle_size - 1)
    near_blocks = [kvd_local]
    for distance in range(1, span + 1):
        near_blocks.append(shifted(kvd_local, "blk", distance))
    flags = [jnp.int32(1)]
    for distance in range(1, span + 1):
        last_segment = near_blocks[distance][block_rows - 1, 2 * kv_cols].astype(jnp.float32)
        flags.append(((my_block - distance >= 0) & (last_segment == first_segment)).astype(jnp.int32))
    flags = jnp.stack(flags)
    near_keys = jnp.stack([kvd[:, :kv_cols] for kvd in near_blocks])
    near_values = jnp.stack([kvd[:, kv_cols : 2 * kv_cols] for kvd in near_blocks])
    near_docs = jnp.stack([kvd[:, 2 * kv_cols].astype(jnp.float32) for kvd in near_blocks])[:, None, :]
    query_total, key_parts, value_parts = block_attention(
        flags,
        packed[:, :q_cols],
        packed[:, q_cols : 2 * q_cols],
        row_terms_blk.transpose(1, 0)[:, :, None],
        query_segment[:, None],
        near_docs,
        near_keys,
        near_values,
    )
    kv_grad = jnp.concatenate([key_parts[0], value_parts[0]], axis=1)
    for distance in range(1, span + 1):
        kv_grad = kv_grad + shifted(
            jnp.concatenate([key_parts[distance], value_parts[distance]], axis=1), "blk", -distance
        )

    query_grad = (query_total * logit_scale).astype(jnp.bfloat16)
    key_gradient = (kv_grad[:, :kv_cols] * logit_scale).astype(jnp.bfloat16)
    value_gradient = kv_grad[:, kv_cols:].astype(jnp.bfloat16)
    out_packed = jnp.concatenate([query_grad, key_gradient, value_gradient], axis=1).reshape(
        head_ways, shard_rows, 1, q_cols + 2 * kv_cols
    )
    out_packed = lax.all_to_all(out_packed, "head", split_axis=0, concat_axis=2, tiled=True)
    out_packed = out_packed.reshape(shard_rows, head_ways, q_cols + 2 * kv_cols)
    return (
        out_packed[:, :, :q_cols].reshape(shard_rows, head_ways * q_cols),
        out_packed[:, :, q_cols : q_cols + kv_cols].reshape(shard_rows, head_ways * kv_cols),
        out_packed[:, :, q_cols + kv_cols :].reshape(shard_rows, head_ways * kv_cols),
    )


def solution(mesh):
    return jax.shard_map(
        per_device,
        mesh=mesh,
        in_specs=(
            P(("blk", "head"), None),
            P(("blk", "head"), None),
            P(("blk", "head"), None),
            P(("blk", "head"), None),
            P(("blk", "head"), None),
            P(("blk", "head")),
        ),
        out_specs=(P(("blk", "head"), None), P(("blk", "head"), None), P(("blk", "head"), None)),
        check_vma=False,
    )
```

```python
import functools

import jax
import jax.numpy as jnp
from jax import lax
from jax.experimental import pallas as pl
from jax.experimental.pallas import tpu as pltpu
from jax.sharding import PartitionSpec as P

HEAD_WIDTH = 128
DOC_SPAN = 4


masked_score = -1e30


def shifted(block, axis, distance):
    devices = range(lax.axis_size(axis))
    route = [(i - distance, i) for i in devices if i - distance in devices]
    return lax.ppermute(block, axis, route)


def attn_kernel(flags_ref, q_ref, do_ref, rt_ref, qdoc_ref, kdoc_ref, k_ref, v_ref,
                dq_ref, dk_ref, dv_ref, m_ref, l_ref, *, n_near, logit_scale):
    head = pl.program_id(0)
    rows = q_ref.shape[0]

    @pl.when(head == 0)
    def _():
        dk_ref[...] = jnp.zeros_like(dk_ref)
        dv_ref[...] = jnp.zeros_like(dv_ref)

    q = q_ref[...]
    do = do_ref[...]
    qdoc = qdoc_ref[...]
    row_id = lax.broadcasted_iota(jnp.int32, (rows, rows), 0)
    col_id = lax.broadcasted_iota(jnp.int32, (rows, rows), 1)

    def allowed_of(d):
        same = qdoc == kdoc_ref[d]
        if d == 0:
            same = same & (col_id <= row_id)
        return same

    def scores_of(d):
        s = lax.dot_general(q, k_ref[d], (((1,), (1,)), ((), ())),
                            preferred_element_type=jnp.float32) * logit_scale
        return s

    m_ref[...] = jnp.full(m_ref.shape, masked_score, jnp.float32)
    l_ref[...] = jnp.zeros(l_ref.shape, jnp.float32)
    for d in range(n_near):
        @pl.when(flags_ref[d] > 0)
        def _():
            allowed = allowed_of(d)
            s = jnp.where(allowed, scores_of(d), masked_score)
            m_old = m_ref[...]
            m_new = jnp.maximum(m_old, jnp.max(s, axis=-1, keepdims=True))
            l_ref[...] = l_ref[...] * jnp.exp(m_old - m_new) + jnp.sum(
                jnp.where(allowed, jnp.exp(s - m_new), 0.0), axis=-1, keepdims=True)
            m_ref[...] = m_new

    log_total = m_ref[...] + jnp.log(l_ref[...])
    rt = rt_ref[0]
    dq_ref[...] = jnp.zeros_like(dq_ref)
    for d in range(n_near):
        @pl.when(flags_ref[d] > 0)
        def _():
            allowed = allowed_of(d)
            s = scores_of(d)
            p = jnp.where(allowed, jnp.exp(s - log_total), 0.0)
            dp = lax.dot_general(do, v_ref[d], (((1,), (1,)), ((), ())),
                                 preferred_element_type=jnp.float32)
            ds = (p * (dp - rt)).astype(jnp.bfloat16)
            pb = p.astype(jnp.bfloat16)
            dv_ref[d] += lax.dot_general(pb, do, (((0,), (0,)), ((), ())),
                                         preferred_element_type=jnp.float32)
            dk_ref[d] += lax.dot_general(ds, q, (((0,), (0,)), ((), ())),
                                         preferred_element_type=jnp.float32)
            dq_ref[...] += jnp.dot(ds, k_ref[d], preferred_element_type=jnp.float32)


def block_attention(flags, q, do, rt, qdoc, kdoc, k, v):
    rows, cols = q.shape
    heads = cols // HEAD_WIDTH
    n_near = k.shape[0]
    kern = functools.partial(attn_kernel, n_near=n_near, logit_scale=HEAD_WIDTH ** (-0.5))
    full3 = lambda shape: pl.BlockSpec(shape, lambda h, f: (0, 0, 0))
    flops = 2 * heads * n_near * rows * rows * HEAD_WIDTH * 6
    return pl.pallas_call(
        kern,
        out_shape=(
            jax.ShapeDtypeStruct((rows, cols), jnp.float32),
            jax.ShapeDtypeStruct((n_near, rows, HEAD_WIDTH), jnp.float32),
            jax.ShapeDtypeStruct((n_near, rows, HEAD_WIDTH), jnp.float32),
        ),
        grid_spec=pltpu.PrefetchScalarGridSpec(
            num_scalar_prefetch=1,
            grid=(heads,),
            in_specs=[
                pl.BlockSpec((rows, HEAD_WIDTH), lambda h, f: (0, h)),
                pl.BlockSpec((rows, HEAD_WIDTH), lambda h, f: (0, h)),
                pl.BlockSpec((1, rows, 1), lambda h, f: (h, 0, 0)),
                pl.BlockSpec((rows, 1), lambda h, f: (0, 0)),
                full3((n_near, 1, rows)),
                full3((n_near, rows, HEAD_WIDTH)),
                full3((n_near, rows, HEAD_WIDTH)),
            ],
            out_specs=[
                pl.BlockSpec((rows, HEAD_WIDTH), lambda h, f: (0, h)),
                full3((n_near, rows, HEAD_WIDTH)),
                full3((n_near, rows, HEAD_WIDTH)),
            ],
            scratch_shapes=[pltpu.VMEM((rows, 1), jnp.float32), pltpu.VMEM((rows, 1), jnp.float32)],
        ),
        compiler_params=pltpu.CompilerParams(dimension_semantics=("arbitrary",)),
        cost_estimate=pl.CostEstimate(flops=flops, transcendentals=2 * heads * n_near * rows * rows,
                                      bytes_accessed=4 * rows * cols * 2 + 8 * n_near * rows * HEAD_WIDTH * 2),
    )(flags, q, do, rt, qdoc, kdoc, k, v)


def per_device(query_matrix, key_matrix, value_matrix, output_cotangent, forward_output, doc_ids):
    cycle_size = lax.axis_size("blk")
    head_ways = lax.axis_size("head")
    shard_rows = query_matrix.shape[0]
    block_rows = shard_rows * head_ways
    query_heads = query_matrix.shape[1] // (HEAD_WIDTH * head_ways)
    kv_heads = key_matrix.shape[1] // (HEAD_WIDTH * head_ways)
    heads_per_group = query_heads // kv_heads
    q_cols = query_heads * HEAD_WIDTH
    kv_cols = kv_heads * HEAD_WIDTH
    logit_scale = HEAD_WIDTH ** (-0.5)
    all_heads = query_matrix.shape[1] // HEAD_WIDTH

    row_terms_local = jnp.sum(
        output_cotangent.astype(jnp.float32).reshape(shard_rows, all_heads, HEAD_WIDTH)
        * forward_output.astype(jnp.float32).reshape(shard_rows, all_heads, HEAD_WIDTH),
        axis=-1,
    ).reshape(shard_rows, head_ways, query_heads)
    doc_half = jnp.broadcast_to(
        doc_ids.astype(jnp.bfloat16)[:, None, None], (shard_rows, head_ways, HEAD_WIDTH)
    )
    kvd_local = jnp.concatenate(
        [
            key_matrix.reshape(shard_rows, head_ways, kv_cols),
            value_matrix.reshape(shard_rows, head_ways, kv_cols),
            doc_half,
        ],
        axis=2,
    )
    kvd_local = lax.all_to_all(kvd_local, "head", split_axis=1, concat_axis=0, tiled=True)
    kvd_local = kvd_local.reshape(block_rows, 2 * kv_cols + HEAD_WIDTH)
    row_terms_blk = lax.all_to_all(
        row_terms_local, "head", split_axis=1, concat_axis=0, tiled=True
    ).reshape(block_rows, query_heads)
    packed = jnp.concatenate(
        [
            query_matrix.reshape(shard_rows, head_ways, q_cols),
            output_cotangent.reshape(shard_rows, head_ways, q_cols),
        ],
        axis=2,
    )
    packed = lax.all_to_all(packed, "head", split_axis=1, concat_axis=0, tiled=True)
    packed = packed.reshape(block_rows, 2 * q_cols)

    my_block = lax.axis_index("blk")
    query_segment = kvd_local[:, 2 * kv_cols].astype(jnp.float32)
    first_segment = query_segment[0]

    span = min(DOC_SPAN, cycle_size - 1)
    near_blocks = [kvd_local]
    for distance in range(1, span + 1):
        near_blocks.append(shifted(kvd_local, "blk", distance))
    flags = [jnp.int32(1)]
    for distance in range(1, span + 1):
        last_segment = near_blocks[distance][block_rows - 1, 2 * kv_cols].astype(jnp.float32)
        flags.append(((my_block - distance >= 0) & (last_segment == first_segment)).astype(jnp.int32))
    flags = jnp.stack(flags)
    near_keys = jnp.stack([kvd[:, :kv_cols] for kvd in near_blocks])
    near_values = jnp.stack([kvd[:, kv_cols : 2 * kv_cols] for kvd in near_blocks])
    near_docs = jnp.stack([kvd[:, 2 * kv_cols].astype(jnp.float32) for kvd in near_blocks])[:, None, :]
    query_total, key_parts, value_parts = block_attention(
        flags,
        packed[:, :q_cols],
        packed[:, q_cols : 2 * q_cols],
        row_terms_blk.transpose(1, 0)[:, :, None],
        query_segment[:, None],
        near_docs,
        near_keys,
        near_values,
    )
    query_grad = (query_total * logit_scale).astype(jnp.bfloat16).reshape(
        head_ways, shard_rows, 1, q_cols
    )
    query_grad = lax.all_to_all(query_grad, "head", split_axis=0, concat_axis=2, tiled=True)
    kv_grad = jnp.concatenate([key_parts[0], value_parts[0]], axis=1)
    for distance in range(1, span + 1):
        sent = jnp.concatenate([key_parts[distance], value_parts[distance]], axis=1)
        kv_grad = kv_grad + shifted(sent.astype(jnp.bfloat16), "blk", -distance).astype(
            jnp.float32
        )
    key_gradient = (kv_grad[:, :kv_cols] * logit_scale).astype(jnp.bfloat16)
    value_gradient = kv_grad[:, kv_cols:].astype(jnp.bfloat16)
    out_packed = jnp.concatenate([key_gradient, value_gradient], axis=1).reshape(
        head_ways, shard_rows, 1, 2 * kv_cols
    )
    out_packed = lax.all_to_all(out_packed, "head", split_axis=0, concat_axis=2, tiled=True)
    out_packed = out_packed.reshape(shard_rows, head_ways, 2 * kv_cols)
    return (
        query_grad.reshape(shard_rows, head_ways * q_cols),
        out_packed[:, :, :kv_cols].reshape(shard_rows, head_ways * kv_cols),
        out_packed[:, :, kv_cols:].reshape(shard_rows, head_ways * kv_cols),
    )


def solution(mesh):
    return jax.shard_map(
        per_device,
        mesh=mesh,
        in_specs=(
            P(("blk", "head"), None),
            P(("blk", "head"), None),
            P(("blk", "head"), None),
            P(("blk", "head"), None),
            P(("blk", "head"), None),
            P(("blk", "head")),
        ),
        out_specs=(P(("blk", "head"), None), P(("blk", "head"), None), P(("blk", "head"), None)),
        check_vma=False,
    )
```

```python
import functools

import jax
import jax.numpy as jnp
from jax import lax
from jax.experimental import pallas as pl
from jax.experimental.pallas import tpu as pltpu
from jax.sharding import PartitionSpec as P

HEAD_WIDTH = 128
DOC_SPAN = 4


masked_score = -1e30


def shifted(block, axis, distance):
    devices = range(lax.axis_size(axis))
    route = [(i - distance, i) for i in devices if i - distance in devices]
    return lax.ppermute(block, axis, route)


def attn_kernel(flags_ref, q_ref, do_ref, rt_ref, qdoc_ref, kdoc_ref, k_ref, v_ref,
                dq_ref, dk_ref, dv_ref, bias_ref, m_ref, l_ref, *, n_near, logit_scale):
    head = pl.program_id(0)
    rows = q_ref.shape[0]

    @pl.when(head == 0)
    def _():
        dk_ref[...] = jnp.zeros_like(dk_ref)
        dv_ref[...] = jnp.zeros_like(dv_ref)
        key_id = lax.broadcasted_iota(jnp.int32, (rows, rows), 0)
        query_id = lax.broadcasted_iota(jnp.int32, (rows, rows), 1)
        qdoc = qdoc_ref[...]
        for d in range(n_near):
            @pl.when(flags_ref[d] > 0)
            def _():
                allowed = kdoc_ref[d] == qdoc
                if d == 0:
                    allowed = allowed & (key_id <= query_id)
                bias_ref[d] = jnp.where(allowed, 0.0, masked_score)

    q = q_ref[...]
    do = do_ref[...]

    def scores_of(d):
        s = lax.dot_general(k_ref[d], q, (((1,), (1,)), ((), ())),
                            preferred_element_type=jnp.float32)
        return s * logit_scale + bias_ref[d]

    m_ref[...] = jnp.full(m_ref.shape, masked_score, jnp.float32)
    l_ref[...] = jnp.zeros(l_ref.shape, jnp.float32)
    for d in range(n_near):
        @pl.when(flags_ref[d] > 0)
        def _():
            s = scores_of(d)
            m_old = m_ref[...]
            m_new = jnp.maximum(m_old, jnp.max(s, axis=0, keepdims=True))
            l_ref[...] = l_ref[...] * jnp.exp(m_old - m_new) + jnp.sum(
                jnp.exp(s - m_new), axis=0, keepdims=True)
            m_ref[...] = m_new

    log_total = m_ref[...] + jnp.log(l_ref[...])
    rt = rt_ref[0]
    dq_ref[...] = jnp.zeros_like(dq_ref)
    for d in range(n_near):
        @pl.when(flags_ref[d] > 0)
        def _():
            p = jnp.exp(scores_of(d) - log_total)
            dp = lax.dot_general(v_ref[d], do, (((1,), (1,)), ((), ())),
                                 preferred_element_type=jnp.float32)
            ds = (p * (dp - rt)).astype(jnp.bfloat16)
            pb = p.astype(jnp.bfloat16)
            dv_ref[d] += jnp.dot(pb, do, preferred_element_type=jnp.float32)
            dk_ref[d] += jnp.dot(ds, q, preferred_element_type=jnp.float32)
            dq_ref[...] += lax.dot_general(ds, k_ref[d], (((0,), (0,)), ((), ())),
                                           preferred_element_type=jnp.float32)


def block_attention(flags, q, do, rt, qdoc, kdoc, k, v):
    rows, cols = q.shape
    heads = cols // HEAD_WIDTH
    n_near = k.shape[0]
    kern = functools.partial(attn_kernel, n_near=n_near, logit_scale=HEAD_WIDTH ** (-0.5))
    full3 = lambda shape: pl.BlockSpec(shape, lambda h, f: (0, 0, 0))
    flops = 2 * heads * n_near * rows * rows * HEAD_WIDTH * 6
    return pl.pallas_call(
        kern,
        out_shape=(
            jax.ShapeDtypeStruct((rows, cols), jnp.float32),
            jax.ShapeDtypeStruct((n_near, rows, HEAD_WIDTH), jnp.float32),
            jax.ShapeDtypeStruct((n_near, rows, HEAD_WIDTH), jnp.float32),
        ),
        grid_spec=pltpu.PrefetchScalarGridSpec(
            num_scalar_prefetch=1,
            grid=(heads,),
            in_specs=[
                pl.BlockSpec((rows, HEAD_WIDTH), lambda h, f: (0, h)),
                pl.BlockSpec((rows, HEAD_WIDTH), lambda h, f: (0, h)),
                pl.BlockSpec((1, 1, rows), lambda h, f: (h, 0, 0)),
                pl.BlockSpec((1, rows), lambda h, f: (0, 0)),
                full3((n_near, rows, 1)),
                full3((n_near, rows, HEAD_WIDTH)),
                full3((n_near, rows, HEAD_WIDTH)),
            ],
            out_specs=[
                pl.BlockSpec((rows, HEAD_WIDTH), lambda h, f: (0, h)),
                full3((n_near, rows, HEAD_WIDTH)),
                full3((n_near, rows, HEAD_WIDTH)),
            ],
            scratch_shapes=[
                pltpu.VMEM((n_near, rows, rows), jnp.float32),
                pltpu.VMEM((1, rows), jnp.float32),
                pltpu.VMEM((1, rows), jnp.float32),
            ],
        ),
        compiler_params=pltpu.CompilerParams(dimension_semantics=("arbitrary",)),
        cost_estimate=pl.CostEstimate(flops=flops, transcendentals=2 * heads * n_near * rows * rows,
                                      bytes_accessed=4 * rows * cols * 2 + 8 * n_near * rows * HEAD_WIDTH * 2),
    )(flags, q, do, rt, qdoc, kdoc, k, v)


def per_device(query_matrix, key_matrix, value_matrix, output_cotangent, forward_output, doc_ids):
    cycle_size = lax.axis_size("blk")
    head_ways = lax.axis_size("head")
    shard_rows = query_matrix.shape[0]
    block_rows = shard_rows * head_ways
    query_heads = query_matrix.shape[1] // (HEAD_WIDTH * head_ways)
    kv_heads = key_matrix.shape[1] // (HEAD_WIDTH * head_ways)
    heads_per_group = query_heads // kv_heads
    q_cols = query_heads * HEAD_WIDTH
    kv_cols = kv_heads * HEAD_WIDTH
    logit_scale = HEAD_WIDTH ** (-0.5)
    all_heads = query_matrix.shape[1] // HEAD_WIDTH

    row_terms_local = jnp.sum(
        output_cotangent.astype(jnp.float32).reshape(shard_rows, all_heads, HEAD_WIDTH)
        * forward_output.astype(jnp.float32).reshape(shard_rows, all_heads, HEAD_WIDTH),
        axis=-1,
    ).reshape(shard_rows, head_ways, query_heads)
    doc_half = jnp.broadcast_to(
        doc_ids.astype(jnp.bfloat16)[:, None, None], (shard_rows, head_ways, HEAD_WIDTH)
    )
    kvd_local = jnp.concatenate(
        [
            key_matrix.reshape(shard_rows, head_ways, kv_cols),
            value_matrix.reshape(shard_rows, head_ways, kv_cols),
            doc_half,
        ],
        axis=2,
    )
    kvd_local = lax.all_to_all(kvd_local, "head", split_axis=1, concat_axis=0, tiled=True)
    kvd_local = kvd_local.reshape(block_rows, 2 * kv_cols + HEAD_WIDTH)
    row_terms_blk = lax.all_to_all(
        row_terms_local, "head", split_axis=1, concat_axis=0, tiled=True
    ).reshape(block_rows, query_heads)
    packed = jnp.concatenate(
        [
            query_matrix.reshape(shard_rows, head_ways, q_cols),
            output_cotangent.reshape(shard_rows, head_ways, q_cols),
        ],
        axis=2,
    )
    packed = lax.all_to_all(packed, "head", split_axis=1, concat_axis=0, tiled=True)
    packed = packed.reshape(block_rows, 2 * q_cols)

    my_block = lax.axis_index("blk")
    query_segment = kvd_local[:, 2 * kv_cols].astype(jnp.float32)
    first_segment = query_segment[0]

    span = min(DOC_SPAN, cycle_size - 1)
    near_blocks = [kvd_local]
    for distance in range(1, span + 1):
        near_blocks.append(shifted(kvd_local, "blk", distance))
    flags = [jnp.int32(1)]
    for distance in range(1, span + 1):
        last_segment = near_blocks[distance][block_rows - 1, 2 * kv_cols].astype(jnp.float32)
        flags.append(((my_block - distance >= 0) & (last_segment == first_segment)).astype(jnp.int32))
    flags = jnp.stack(flags)
    near_keys = jnp.stack([kvd[:, :kv_cols] for kvd in near_blocks])
    near_values = jnp.stack([kvd[:, kv_cols : 2 * kv_cols] for kvd in near_blocks])
    near_docs = jnp.stack([kvd[:, 2 * kv_cols].astype(jnp.float32) for kvd in near_blocks])[:, :, None]
    query_total, key_parts, value_parts = block_attention(
        flags,
        packed[:, :q_cols],
        packed[:, q_cols : 2 * q_cols],
        row_terms_blk.transpose(1, 0)[:, None, :],
        query_segment[None, :],
        near_docs,
        near_keys,
        near_values,
    )
    query_grad = (query_total * logit_scale).astype(jnp.bfloat16).reshape(
        head_ways, shard_rows, 1, q_cols
    )
    query_grad = lax.all_to_all(query_grad, "head", split_axis=0, concat_axis=2, tiled=True)
    kv_grad = jnp.concatenate([key_parts[0], value_parts[0]], axis=1)
    for distance in range(1, span + 1):
        sent = jnp.concatenate([key_parts[distance], value_parts[distance]], axis=1)
        kv_grad = kv_grad + shifted(sent.astype(jnp.bfloat16), "blk", -distance).astype(
            jnp.float32
        )
    key_gradient = (kv_grad[:, :kv_cols] * logit_scale).astype(jnp.bfloat16)
    value_gradient = kv_grad[:, kv_cols:].astype(jnp.bfloat16)
    out_packed = jnp.concatenate([key_gradient, value_gradient], axis=1).reshape(
        head_ways, shard_rows, 1, 2 * kv_cols
    )
    out_packed = lax.all_to_all(out_packed, "head", split_axis=0, concat_axis=2, tiled=True)
    out_packed = out_packed.reshape(shard_rows, head_ways, 2 * kv_cols)
    return (
        query_grad.reshape(shard_rows, head_ways * q_cols),
        out_packed[:, :, :kv_cols].reshape(shard_rows, head_ways * kv_cols),
        out_packed[:, :, kv_cols:].reshape(shard_rows, head_ways * kv_cols),
    )


def solution(mesh):
    return jax.shard_map(
        per_device,
        mesh=mesh,
        in_specs=(
            P(("blk", "head"), None),
            P(("blk", "head"), None),
            P(("blk", "head"), None),
            P(("blk", "head"), None),
            P(("blk", "head"), None),
            P(("blk", "head")),
        ),
        out_specs=(P(("blk", "head"), None), P(("blk", "head"), None), P(("blk", "head"), None)),
        check_vma=False,
    )
```

```python
import functools

import jax
import jax.numpy as jnp
from jax import lax
from jax.experimental import pallas as pl
from jax.experimental.pallas import tpu as pltpu
from jax.sharding import PartitionSpec as P

HEAD_WIDTH = 128
DOC_SPAN = 4


masked_score = -1e30


def shifted(block, axis, distance):
    devices = range(lax.axis_size(axis))
    route = [(i - distance, i) for i in devices if i - distance in devices]
    return lax.ppermute(block, axis, route)


def attn_kernel(flags_ref, q_ref, do_ref, rt_ref, qdoc_ref, kdoc_ref, k_ref, v_ref,
                dq_ref, dk_ref, dv_ref, bias_ref, m_ref, l_ref, *, n_near, logit_scale):
    head = pl.program_id(0)
    rows = q_ref.shape[0]

    @pl.when(head == 0)
    def _():
        dk_ref[...] = jnp.zeros_like(dk_ref)
        dv_ref[...] = jnp.zeros_like(dv_ref)
        key_id = lax.broadcasted_iota(jnp.int32, (rows, rows), 0)
        query_id = lax.broadcasted_iota(jnp.int32, (rows, rows), 1)
        qdoc = qdoc_ref[...]
        for d in range(n_near):
            @pl.when(flags_ref[d] > 0)
            def _():
                allowed = kdoc_ref[d] == qdoc
                if d == 0:
                    allowed = allowed & (key_id <= query_id)
                bias_ref[d] = jnp.where(allowed, 0.0, masked_score)

    q = q_ref[...]
    do = do_ref[...]

    def scores_of(d):
        s = lax.dot_general(k_ref[d], q, (((1,), (1,)), ((), ())),
                            preferred_element_type=jnp.float32)
        return s * logit_scale + bias_ref[d]

    m_ref[...] = jnp.full(m_ref.shape, masked_score, jnp.float32)
    l_ref[...] = jnp.zeros(l_ref.shape, jnp.float32)
    for d in range(n_near):
        @pl.when(flags_ref[d] > 0)
        def _():
            s = scores_of(d)
            m_old = m_ref[...]
            m_new = jnp.maximum(m_old, jnp.max(s, axis=0, keepdims=True))
            l_ref[...] = l_ref[...] * jnp.exp(m_old - m_new) + jnp.sum(
                jnp.exp(s - m_new), axis=0, keepdims=True)
            m_ref[...] = m_new

    log_total = m_ref[...] + jnp.log(l_ref[...])
    rt = rt_ref[0]
    dq_ref[...] = jnp.zeros_like(dq_ref)
    for d in range(n_near):
        @pl.when(flags_ref[d] > 0)
        def _():
            p = jnp.exp(scores_of(d) - log_total)
            dp = lax.dot_general(v_ref[d], do, (((1,), (1,)), ((), ())),
                                 preferred_element_type=jnp.float32)
            ds = (p * (dp - rt)).astype(jnp.bfloat16)
            pb = p.astype(jnp.bfloat16)
            dv_ref[d] += jnp.dot(pb, do, preferred_element_type=jnp.float32)
            dk_ref[d] += jnp.dot(ds, q, preferred_element_type=jnp.float32)
            dq_ref[...] += lax.dot_general(ds, k_ref[d], (((0,), (0,)), ((), ())),
                                           preferred_element_type=jnp.float32)


def block_attention(flags, q, do, rt, qdoc, kdoc, k, v):
    rows, cols = q.shape
    heads = cols // HEAD_WIDTH
    n_near = k.shape[0]
    kern = functools.partial(attn_kernel, n_near=n_near, logit_scale=HEAD_WIDTH ** (-0.5))
    full3 = lambda shape: pl.BlockSpec(shape, lambda h, f: (0, 0, 0))
    flops = 2 * heads * n_near * rows * rows * HEAD_WIDTH * 6
    return pl.pallas_call(
        kern,
        out_shape=(
            jax.ShapeDtypeStruct((rows, cols), jnp.float32),
            jax.ShapeDtypeStruct((n_near, rows, HEAD_WIDTH), jnp.float32),
            jax.ShapeDtypeStruct((n_near, rows, HEAD_WIDTH), jnp.float32),
        ),
        grid_spec=pltpu.PrefetchScalarGridSpec(
            num_scalar_prefetch=1,
            grid=(heads,),
            in_specs=[
                pl.BlockSpec((rows, HEAD_WIDTH), lambda h, f: (0, h)),
                pl.BlockSpec((rows, HEAD_WIDTH), lambda h, f: (0, h)),
                pl.BlockSpec((1, 1, rows), lambda h, f: (h, 0, 0)),
                pl.BlockSpec((1, rows), lambda h, f: (0, 0)),
                full3((n_near, rows, 1)),
                full3((n_near, rows, HEAD_WIDTH)),
                full3((n_near, rows, HEAD_WIDTH)),
            ],
            out_specs=[
                pl.BlockSpec((rows, HEAD_WIDTH), lambda h, f: (0, h)),
                full3((n_near, rows, HEAD_WIDTH)),
                full3((n_near, rows, HEAD_WIDTH)),
            ],
            scratch_shapes=[
                pltpu.VMEM((n_near, rows, rows), jnp.float32),
                pltpu.VMEM((1, rows), jnp.float32),
                pltpu.VMEM((1, rows), jnp.float32),
            ],
        ),
        compiler_params=pltpu.CompilerParams(dimension_semantics=("arbitrary",)),
        cost_estimate=pl.CostEstimate(flops=flops, transcendentals=2 * heads * n_near * rows * rows,
                                      bytes_accessed=4 * rows * cols * 2 + 8 * n_near * rows * HEAD_WIDTH * 2),
    )(flags, q, do, rt, qdoc, kdoc, k, v)


def per_device(query_matrix, key_matrix, value_matrix, output_cotangent, forward_output, doc_ids):
    cycle_size = lax.axis_size("blk")
    head_ways = lax.axis_size("head")
    shard_rows = query_matrix.shape[0]
    block_rows = shard_rows * head_ways
    query_heads = query_matrix.shape[1] // (HEAD_WIDTH * head_ways)
    kv_heads = key_matrix.shape[1] // (HEAD_WIDTH * head_ways)
    heads_per_group = query_heads // kv_heads
    q_cols = query_heads * HEAD_WIDTH
    kv_cols = kv_heads * HEAD_WIDTH
    logit_scale = HEAD_WIDTH ** (-0.5)
    all_heads = query_matrix.shape[1] // HEAD_WIDTH

    row_terms_local = jnp.sum(
        output_cotangent.astype(jnp.float32).reshape(shard_rows, all_heads, HEAD_WIDTH)
        * forward_output.astype(jnp.float32).reshape(shard_rows, all_heads, HEAD_WIDTH),
        axis=-1,
    ).reshape(shard_rows, head_ways, query_heads)
    terms_parts = []
    remainder = row_terms_local
    for _ in range(3):
        part = lax.reduce_precision(remainder, exponent_bits=8, mantissa_bits=7)
        terms_parts.append(part.astype(jnp.bfloat16))
        remainder = remainder - part
    misc = jnp.concatenate(
        [
            jnp.broadcast_to(doc_ids.astype(jnp.bfloat16)[:, None, None], (shard_rows, head_ways, 1)),
            *terms_parts,
            jnp.zeros((shard_rows, head_ways, HEAD_WIDTH - 1 - 3 * query_heads), jnp.bfloat16),
        ],
        axis=2,
    )
    kvd_local = jnp.concatenate(
        [
            key_matrix.reshape(shard_rows, head_ways, kv_cols),
            value_matrix.reshape(shard_rows, head_ways, kv_cols),
            misc,
        ],
        axis=2,
    )
    kvd_local = lax.all_to_all(kvd_local, "head", split_axis=1, concat_axis=0, tiled=True)
    kvd_local = kvd_local.reshape(block_rows, 2 * kv_cols + HEAD_WIDTH)
    terms_at = 2 * kv_cols + 1
    row_terms_blk = (
        kvd_local[:, terms_at : terms_at + query_heads].astype(jnp.float32)
        + kvd_local[:, terms_at + query_heads : terms_at + 2 * query_heads].astype(jnp.float32)
    ) + kvd_local[:, terms_at + 2 * query_heads : terms_at + 3 * query_heads].astype(jnp.float32)
    packed = jnp.concatenate(
        [
            query_matrix.reshape(shard_rows, head_ways, q_cols),
            output_cotangent.reshape(shard_rows, head_ways, q_cols),
        ],
        axis=2,
    )
    packed = lax.all_to_all(packed, "head", split_axis=1, concat_axis=0, tiled=True)
    packed = packed.reshape(block_rows, 2 * q_cols)

    my_block = lax.axis_index("blk")
    query_segment = kvd_local[:, 2 * kv_cols].astype(jnp.float32)
    first_segment = query_segment[0]

    span = min(DOC_SPAN, cycle_size - 1)
    near_blocks = [kvd_local]
    for distance in range(1, span + 1):
        near_blocks.append(shifted(kvd_local, "blk", distance))
    flags = [jnp.int32(1)]
    for distance in range(1, span + 1):
        last_segment = near_blocks[distance][block_rows - 1, 2 * kv_cols].astype(jnp.float32)
        flags.append(((my_block - distance >= 0) & (last_segment == first_segment)).astype(jnp.int32))
    flags = jnp.stack(flags)
    near_keys = jnp.stack([kvd[:, :kv_cols] for kvd in near_blocks])
    near_values = jnp.stack([kvd[:, kv_cols : 2 * kv_cols] for kvd in near_blocks])
    near_docs = jnp.stack([kvd[:, 2 * kv_cols].astype(jnp.float32) for kvd in near_blocks])[:, :, None]
    query_total, key_parts, value_parts = block_attention(
        flags,
        packed[:, :q_cols],
        packed[:, q_cols : 2 * q_cols],
        row_terms_blk.transpose(1, 0)[:, None, :],
        query_segment[None, :],
        near_docs,
        near_keys,
        near_values,
    )
    my_group = lax.axis_index("head")
    query_grad = (query_total * logit_scale).astype(jnp.bfloat16)
    query_out = jnp.zeros((shard_rows, head_ways * q_cols), jnp.bfloat16)
    for step in range(head_ways):
        target = (my_group + step) % head_ways
        piece = lax.dynamic_slice_in_dim(query_grad, target * shard_rows, shard_rows, 0)
        if step > 0:
            piece = lax.ppermute(
                piece, "head", [(i, (i + step) % head_ways) for i in range(head_ways)]
            )
        source = (my_group - step) % head_ways
        query_out = lax.dynamic_update_slice_in_dim(query_out, piece, source * q_cols, 1)
    kv_grad = jnp.concatenate([key_parts[0], value_parts[0]], axis=1)
    for distance in range(1, span + 1):
        sent = jnp.concatenate([key_parts[distance], value_parts[distance]], axis=1)
        kv_grad = kv_grad + shifted(sent.astype(jnp.bfloat16), "blk", -distance).astype(
            jnp.float32
        )
    key_gradient = (kv_grad[:, :kv_cols] * logit_scale).astype(jnp.bfloat16)
    value_gradient = kv_grad[:, kv_cols:].astype(jnp.bfloat16)
    out_packed = jnp.concatenate([key_gradient, value_gradient], axis=1).reshape(
        head_ways, shard_rows, 1, 2 * kv_cols
    )
    out_packed = lax.all_to_all(out_packed, "head", split_axis=0, concat_axis=2, tiled=True)
    out_packed = out_packed.reshape(shard_rows, head_ways, 2 * kv_cols)
    return (
        query_out,
        out_packed[:, :, :kv_cols].reshape(shard_rows, head_ways * kv_cols),
        out_packed[:, :, kv_cols:].reshape(shard_rows, head_ways * kv_cols),
    )


def solution(mesh):
    return jax.shard_map(
        per_device,
        mesh=mesh,
        in_specs=(
            P(("blk", "head"), None),
            P(("blk", "head"), None),
            P(("blk", "head"), None),
            P(("blk", "head"), None),
            P(("blk", "head"), None),
            P(("blk", "head")),
        ),
        out_specs=(P(("blk", "head"), None), P(("blk", "head"), None), P(("blk", "head"), None)),
        check_vma=False,
    )
```

```python
import functools

import jax
import jax.numpy as jnp
from jax import lax
from jax.experimental import pallas as pl
from jax.experimental.pallas import tpu as pltpu
from jax.sharding import PartitionSpec as P

HEAD_WIDTH = 128
DOC_SPAN = 4


masked_score = -1e30


def shifted(block, axis, distance):
    devices = range(lax.axis_size(axis))
    route = [(i - distance, i) for i in devices if i - distance in devices]
    return lax.ppermute(block, axis, route)


def attn_kernel(flags_ref, q_ref, do_ref, rt_ref, qdoc_ref, kdoc_ref, k_ref, v_ref,
                dq_ref, dk_ref, dv_ref, bias_ref, m_ref, l_ref, *, n_near, logit_scale):
    head = pl.program_id(0)
    rows = q_ref.shape[0]

    @pl.when(head == 0)
    def _():
        dk_ref[...] = jnp.zeros_like(dk_ref)
        dv_ref[...] = jnp.zeros_like(dv_ref)
        key_id = lax.broadcasted_iota(jnp.int32, (rows, rows), 0)
        query_id = lax.broadcasted_iota(jnp.int32, (rows, rows), 1)
        qdoc = qdoc_ref[...]
        for d in range(n_near):
            @pl.when(flags_ref[d] > 0)
            def _():
                allowed = kdoc_ref[d] == qdoc
                if d == 0:
                    allowed = allowed & (key_id <= query_id)
                bias_ref[d] = jnp.where(allowed, 0.0, masked_score)

    q = q_ref[...]
    do = do_ref[...]

    def scores_of(d):
        s = lax.dot_general(k_ref[d], q, (((1,), (1,)), ((), ())),
                            preferred_element_type=jnp.float32)
        return s * logit_scale + bias_ref[d]

    m_ref[...] = jnp.full(m_ref.shape, masked_score, jnp.float32)
    l_ref[...] = jnp.zeros(l_ref.shape, jnp.float32)
    for d in range(n_near):
        @pl.when(flags_ref[d] > 0)
        def _():
            s = scores_of(d)
            m_old = m_ref[...]
            m_new = jnp.maximum(m_old, jnp.max(s, axis=0, keepdims=True))
            l_ref[...] = l_ref[...] * jnp.exp(m_old - m_new) + jnp.sum(
                jnp.exp(s - m_new), axis=0, keepdims=True)
            m_ref[...] = m_new

    log_total = m_ref[...] + jnp.log(l_ref[...])
    rt = rt_ref[0]
    dq_ref[...] = jnp.zeros_like(dq_ref)
    for d in range(n_near):
        @pl.when(flags_ref[d] > 0)
        def _():
            p = jnp.exp(scores_of(d) - log_total)
            dp = lax.dot_general(v_ref[d], do, (((1,), (1,)), ((), ())),
                                 preferred_element_type=jnp.float32)
            ds = (p * (dp - rt)).astype(jnp.bfloat16)
            pb = p.astype(jnp.bfloat16)
            dv_ref[d] += jnp.dot(pb, do, preferred_element_type=jnp.float32)
            dk_ref[d] += jnp.dot(ds, q, preferred_element_type=jnp.float32)
            dq_ref[...] += lax.dot_general(ds, k_ref[d], (((0,), (0,)), ((), ())),
                                           preferred_element_type=jnp.float32)


def block_attention(flags, q, do, rt, qdoc, kdoc, k, v):
    rows, cols = q.shape
    heads = cols // HEAD_WIDTH
    n_near = k.shape[0]
    kern = functools.partial(attn_kernel, n_near=n_near, logit_scale=HEAD_WIDTH ** (-0.5))
    full3 = lambda shape: pl.BlockSpec(shape, lambda h, f: (0, 0, 0))
    flops = 2 * heads * n_near * rows * rows * HEAD_WIDTH * 6
    return pl.pallas_call(
        kern,
        out_shape=(
            jax.ShapeDtypeStruct((rows, cols), jnp.float32),
            jax.ShapeDtypeStruct((n_near, rows, HEAD_WIDTH), jnp.float32),
            jax.ShapeDtypeStruct((n_near, rows, HEAD_WIDTH), jnp.float32),
        ),
        grid_spec=pltpu.PrefetchScalarGridSpec(
            num_scalar_prefetch=1,
            grid=(heads,),
            in_specs=[
                pl.BlockSpec((rows, HEAD_WIDTH), lambda h, f: (0, h)),
                pl.BlockSpec((rows, HEAD_WIDTH), lambda h, f: (0, h)),
                pl.BlockSpec((1, 1, rows), lambda h, f: (h, 0, 0)),
                pl.BlockSpec((1, rows), lambda h, f: (0, 0)),
                full3((n_near, rows, 1)),
                full3((n_near, rows, HEAD_WIDTH)),
                full3((n_near, rows, HEAD_WIDTH)),
            ],
            out_specs=[
                pl.BlockSpec((rows, HEAD_WIDTH), lambda h, f: (0, h)),
                full3((n_near, rows, HEAD_WIDTH)),
                full3((n_near, rows, HEAD_WIDTH)),
            ],
            scratch_shapes=[
                pltpu.VMEM((n_near, rows, rows), jnp.float32),
                pltpu.VMEM((1, rows), jnp.float32),
                pltpu.VMEM((1, rows), jnp.float32),
            ],
        ),
        compiler_params=pltpu.CompilerParams(dimension_semantics=("arbitrary",)),
        cost_estimate=pl.CostEstimate(flops=flops, transcendentals=2 * heads * n_near * rows * rows,
                                      bytes_accessed=4 * rows * cols * 2 + 8 * n_near * rows * HEAD_WIDTH * 2),
    )(flags, q, do, rt, qdoc, kdoc, k, v)


def per_device(query_matrix, key_matrix, value_matrix, output_cotangent, forward_output, doc_ids):
    cycle_size = lax.axis_size("blk")
    head_ways = lax.axis_size("head")
    shard_rows = query_matrix.shape[0]
    block_rows = shard_rows * head_ways
    query_heads = query_matrix.shape[1] // (HEAD_WIDTH * head_ways)
    kv_heads = key_matrix.shape[1] // (HEAD_WIDTH * head_ways)
    heads_per_group = query_heads // kv_heads
    q_cols = query_heads * HEAD_WIDTH
    kv_cols = kv_heads * HEAD_WIDTH
    logit_scale = HEAD_WIDTH ** (-0.5)
    all_heads = query_matrix.shape[1] // HEAD_WIDTH

    row_terms_local = jnp.sum(
        output_cotangent.astype(jnp.float32).reshape(shard_rows, all_heads, HEAD_WIDTH)
        * forward_output.astype(jnp.float32).reshape(shard_rows, all_heads, HEAD_WIDTH),
        axis=-1,
    ).reshape(shard_rows, head_ways, query_heads)
    terms_parts = []
    remainder = row_terms_local
    for _ in range(3):
        part = lax.reduce_precision(remainder, exponent_bits=8, mantissa_bits=7)
        terms_parts.append(part.astype(jnp.bfloat16))
        remainder = remainder - part
    misc = jnp.concatenate(
        [
            jnp.broadcast_to(doc_ids.astype(jnp.bfloat16)[:, None, None], (shard_rows, head_ways, 1)),
            *terms_parts,
            jnp.zeros((shard_rows, head_ways, HEAD_WIDTH - 1 - 3 * query_heads), jnp.bfloat16),
        ],
        axis=2,
    )
    kvd_local = jnp.concatenate(
        [
            key_matrix.reshape(shard_rows, head_ways, kv_cols),
            value_matrix.reshape(shard_rows, head_ways, kv_cols),
            misc,
        ],
        axis=2,
    )
    my_group = lax.axis_index("head")
    kvd_shard = kvd_local
    kvd_local = jnp.zeros((block_rows, 2 * kv_cols + HEAD_WIDTH), jnp.bfloat16)
    for step in range(head_ways):
        target = (my_group + step) % head_ways
        piece = lax.dynamic_index_in_dim(kvd_shard, target, 1, keepdims=False)
        if step > 0:
            piece = lax.ppermute(
                piece, "head", [(i, (i + step) % head_ways) for i in range(head_ways)]
            )
        source = (my_group - step) % head_ways
        kvd_local = lax.dynamic_update_slice_in_dim(kvd_local, piece, source * shard_rows, 0)
    terms_at = 2 * kv_cols + 1
    row_terms_blk = (
        kvd_local[:, terms_at : terms_at + query_heads].astype(jnp.float32)
        + kvd_local[:, terms_at + query_heads : terms_at + 2 * query_heads].astype(jnp.float32)
    ) + kvd_local[:, terms_at + 2 * query_heads : terms_at + 3 * query_heads].astype(jnp.float32)
    packed = jnp.concatenate(
        [
            query_matrix.reshape(shard_rows, head_ways, q_cols),
            output_cotangent.reshape(shard_rows, head_ways, q_cols),
        ],
        axis=2,
    )
    packed = lax.all_to_all(packed, "head", split_axis=1, concat_axis=0, tiled=True)
    packed = packed.reshape(block_rows, 2 * q_cols)

    my_block = lax.axis_index("blk")
    query_segment = kvd_local[:, 2 * kv_cols].astype(jnp.float32)
    first_segment = query_segment[0]

    span = min(DOC_SPAN, cycle_size - 1)
    near_blocks = [kvd_local]
    for distance in range(1, span + 1):
        near_blocks.append(shifted(kvd_local, "blk", distance))
    flags = [jnp.int32(1)]
    for distance in range(1, span + 1):
        last_segment = near_blocks[distance][block_rows - 1, 2 * kv_cols].astype(jnp.float32)
        flags.append(((my_block - distance >= 0) & (last_segment == first_segment)).astype(jnp.int32))
    flags = jnp.stack(flags)
    near_keys = jnp.stack([kvd[:, :kv_cols] for kvd in near_blocks])
    near_values = jnp.stack([kvd[:, kv_cols : 2 * kv_cols] for kvd in near_blocks])
    near_docs = jnp.stack([kvd[:, 2 * kv_cols].astype(jnp.float32) for kvd in near_blocks])[:, :, None]
    query_total, key_parts, value_parts = block_attention(
        flags,
        packed[:, :q_cols],
        packed[:, q_cols : 2 * q_cols],
        row_terms_blk.transpose(1, 0)[:, None, :],
        query_segment[None, :],
        near_docs,
        near_keys,
        near_values,
    )
    query_grad = (query_total * logit_scale).astype(jnp.bfloat16)
    query_out = jnp.zeros((shard_rows, head_ways * q_cols), jnp.bfloat16)
    for step in range(head_ways):
        target = (my_group + step) % head_ways
        piece = lax.dynamic_slice_in_dim(query_grad, target * shard_rows, shard_rows, 0)
        if step > 0:
            piece = lax.ppermute(
                piece, "head", [(i, (i + step) % head_ways) for i in range(head_ways)]
            )
        source = (my_group - step) % head_ways
        query_out = lax.dynamic_update_slice_in_dim(query_out, piece, source * q_cols, 1)
    kv_grad = jnp.concatenate([key_parts[0], value_parts[0]], axis=1)
    for distance in range(1, span + 1):
        sent = jnp.concatenate([key_parts[distance], value_parts[distance]], axis=1)
        kv_grad = kv_grad + shifted(sent.astype(jnp.bfloat16), "blk", -distance).astype(
            jnp.float32
        )
    key_gradient = (kv_grad[:, :kv_cols] * logit_scale).astype(jnp.bfloat16)
    value_gradient = kv_grad[:, kv_cols:].astype(jnp.bfloat16)
    out_packed = jnp.concatenate([key_gradient, value_gradient], axis=1).reshape(
        head_ways, shard_rows, 1, 2 * kv_cols
    )
    out_packed = lax.all_to_all(out_packed, "head", split_axis=0, concat_axis=2, tiled=True)
    out_packed = out_packed.reshape(shard_rows, head_ways, 2 * kv_cols)
    return (
        query_out,
        out_packed[:, :, :kv_cols].reshape(shard_rows, head_ways * kv_cols),
        out_packed[:, :, kv_cols:].reshape(shard_rows, head_ways * kv_cols),
    )


def solution(mesh):
    return jax.shard_map(
        per_device,
        mesh=mesh,
        in_specs=(
            P(("blk", "head"), None),
            P(("blk", "head"), None),
            P(("blk", "head"), None),
            P(("blk", "head"), None),
            P(("blk", "head"), None),
            P(("blk", "head")),
        ),
        out_specs=(P(("blk", "head"), None), P(("blk", "head"), None), P(("blk", "head"), None)),
        check_vma=False,
    )
```

```python
import functools

import jax
import jax.numpy as jnp
from jax import lax
from jax.experimental import pallas as pl
from jax.experimental.pallas import tpu as pltpu
from jax.sharding import PartitionSpec as P

HEAD_WIDTH = 128
DOC_SPAN = 4
TILE = 256


masked_score = -1e30


def shifted(block, axis, distance):
    devices = range(lax.axis_size(axis))
    route = [(i - distance, i) for i in devices if i - distance in devices]
    return lax.ppermute(block, axis, route)


def tile_order(n_near, n_tiles, query_tile):
    order = [(0, query_tile)] + [(0, key_tile) for key_tile in range(query_tile)]
    for d in range(1, n_near):
        order += [(d, key_tile) for key_tile in range(n_tiles)]
    return order


def attn_kernel(flags_ref, q_ref, do_ref, rt_ref, qdoc_ref, kdoc_ref, k_ref, v_ref,
                dq_ref, dk_ref, dv_ref, bias_ref, m_ref, l_ref, *, n_near, logit_scale):
    head = pl.program_id(0)
    rows = q_ref.shape[0]
    n_tiles = rows // TILE

    def flag(d, key_tile, query_tile):
        return flags_ref[(d * n_tiles + key_tile) * n_tiles + query_tile] > 0

    def when_active(d, key_tile, query_tile):
        if d == 0 and key_tile == query_tile:
            return lambda body: body()
        return pl.when(flag(d, key_tile, query_tile))

    def span(t):
        return pl.ds(t * TILE, TILE)

    all_tiles = [(d, kt, qt) for qt in range(n_tiles) for d, kt in tile_order(n_near, n_tiles, qt)]

    @pl.when(head == 0)
    def _():
        dk_ref[...] = jnp.zeros_like(dk_ref)
        dv_ref[...] = jnp.zeros_like(dv_ref)
        key_id = lax.broadcasted_iota(jnp.int32, (TILE, TILE), 0)
        query_id = lax.broadcasted_iota(jnp.int32, (TILE, TILE), 1)
        for d, kt, qt in all_tiles:
            @when_active(d, kt, qt)
            def _():
                allowed = kdoc_ref[d, span(kt), :] == qdoc_ref[:, span(qt)]
                if d == 0 and kt == qt:
                    allowed = allowed & (key_id <= query_id)
                bias_ref[d, span(kt), span(qt)] = jnp.where(allowed, 0.0, masked_score)

    def scores_of(d, kt, qt):
        s = lax.dot_general(k_ref[d, span(kt), :], q_ref[span(qt), :], (((1,), (1,)), ((), ())),
                            preferred_element_type=jnp.float32)
        return s * logit_scale + bias_ref[d, span(kt), span(qt)]

    m_ref[...] = jnp.full(m_ref.shape, masked_score, jnp.float32)
    l_ref[...] = jnp.zeros(l_ref.shape, jnp.float32)
    for d, kt, qt in all_tiles:
        @when_active(d, kt, qt)
        def _():
            s = scores_of(d, kt, qt)
            m_old = m_ref[:, span(qt)]
            m_new = jnp.maximum(m_old, jnp.max(s, axis=0, keepdims=True))
            l_ref[:, span(qt)] = l_ref[:, span(qt)] * jnp.exp(m_old - m_new) + jnp.sum(
                jnp.exp(s - m_new), axis=0, keepdims=True)
            m_ref[:, span(qt)] = m_new

    m_ref[...] = m_ref[...] + jnp.log(l_ref[...])
    dq_ref[...] = jnp.zeros_like(dq_ref)
    for d, kt, qt in all_tiles:
        @when_active(d, kt, qt)
        def _():
            q = q_ref[span(qt), :]
            do = do_ref[span(qt), :]
            p = jnp.exp(scores_of(d, kt, qt) - m_ref[:, span(qt)])
            dp = lax.dot_general(v_ref[d, span(kt), :], do, (((1,), (1,)), ((), ())),
                                 preferred_element_type=jnp.float32)
            ds = (p * (dp - rt_ref[0, :, span(qt)])).astype(jnp.bfloat16)
            pb = p.astype(jnp.bfloat16)
            dv_ref[d, span(kt), :] += jnp.dot(pb, do, preferred_element_type=jnp.float32)
            dk_ref[d, span(kt), :] += jnp.dot(ds, q, preferred_element_type=jnp.float32)
            dq_ref[span(qt), :] += lax.dot_general(ds, k_ref[d, span(kt), :], (((0,), (0,)), ((), ())),
                                                   preferred_element_type=jnp.float32)


def tile_flags(block_flags, qdoc, kdoc):
    n_near, rows = kdoc.shape
    n_tiles = rows // TILE
    first_query = qdoc.reshape(n_tiles, TILE)[:, 0]
    last_key = kdoc.reshape(n_near, n_tiles, TILE)[:, :, TILE - 1]
    touch = last_key[:, :, None] == first_query[None, None, :]
    key_tile = jnp.arange(n_tiles)[:, None]
    query_tile = jnp.arange(n_tiles)[None, :]
    own = (key_tile == query_tile) | ((key_tile < query_tile) & touch[0])
    rest = touch[1:] & (block_flags[1:, None, None] > 0)
    return jnp.concatenate([own[None], rest], axis=0).astype(jnp.int32).reshape(-1)


def block_attention(flags, q, do, rt, qdoc, kdoc, k, v):
    rows, cols = q.shape
    heads = cols // HEAD_WIDTH
    n_near = k.shape[0]
    kern = functools.partial(attn_kernel, n_near=n_near, logit_scale=HEAD_WIDTH ** (-0.5))
    full3 = lambda shape: pl.BlockSpec(shape, lambda h, f: (0, 0, 0))
    flops = 2 * heads * n_near * rows * rows * HEAD_WIDTH * 6
    return pl.pallas_call(
        kern,
        out_shape=(
            jax.ShapeDtypeStruct((rows, cols), jnp.float32),
            jax.ShapeDtypeStruct((n_near, rows, HEAD_WIDTH), jnp.float32),
            jax.ShapeDtypeStruct((n_near, rows, HEAD_WIDTH), jnp.float32),
        ),
        grid_spec=pltpu.PrefetchScalarGridSpec(
            num_scalar_prefetch=1,
            grid=(heads,),
            in_specs=[
                pl.BlockSpec((rows, HEAD_WIDTH), lambda h, f: (0, h)),
                pl.BlockSpec((rows, HEAD_WIDTH), lambda h, f: (0, h)),
                pl.BlockSpec((1, 1, rows), lambda h, f: (h, 0, 0)),
                pl.BlockSpec((1, rows), lambda h, f: (0, 0)),
                full3((n_near, rows, 1)),
                full3((n_near, rows, HEAD_WIDTH)),
                full3((n_near, rows, HEAD_WIDTH)),
            ],
            out_specs=[
                pl.BlockSpec((rows, HEAD_WIDTH), lambda h, f: (0, h)),
                full3((n_near, rows, HEAD_WIDTH)),
                full3((n_near, rows, HEAD_WIDTH)),
            ],
            scratch_shapes=[
                pltpu.VMEM((n_near, rows, rows), jnp.float32),
                pltpu.VMEM((1, rows), jnp.float32),
                pltpu.VMEM((1, rows), jnp.float32),
            ],
        ),
        compiler_params=pltpu.CompilerParams(dimension_semantics=("arbitrary",)),
        cost_estimate=pl.CostEstimate(flops=flops, transcendentals=2 * heads * n_near * rows * rows,
                                      bytes_accessed=4 * rows * cols * 2 + 8 * n_near * rows * HEAD_WIDTH * 2),
    )(flags, q, do, rt, qdoc, kdoc, k, v)


def per_device(query_matrix, key_matrix, value_matrix, output_cotangent, forward_output, doc_ids):
    cycle_size = lax.axis_size("blk")
    head_ways = lax.axis_size("head")
    shard_rows = query_matrix.shape[0]
    block_rows = shard_rows * head_ways
    query_heads = query_matrix.shape[1] // (HEAD_WIDTH * head_ways)
    kv_heads = key_matrix.shape[1] // (HEAD_WIDTH * head_ways)
    heads_per_group = query_heads // kv_heads
    q_cols = query_heads * HEAD_WIDTH
    kv_cols = kv_heads * HEAD_WIDTH
    logit_scale = HEAD_WIDTH ** (-0.5)
    all_heads = query_matrix.shape[1] // HEAD_WIDTH

    row_terms_local = jnp.sum(
        output_cotangent.astype(jnp.float32).reshape(shard_rows, all_heads, HEAD_WIDTH)
        * forward_output.astype(jnp.float32).reshape(shard_rows, all_heads, HEAD_WIDTH),
        axis=-1,
    ).reshape(shard_rows, head_ways, query_heads)
    terms_parts = []
    remainder = row_terms_local
    for _ in range(3):
        part = lax.reduce_precision(remainder, exponent_bits=8, mantissa_bits=7)
        terms_parts.append(part.astype(jnp.bfloat16))
        remainder = remainder - part
    misc = jnp.concatenate(
        [
            jnp.broadcast_to(doc_ids.astype(jnp.bfloat16)[:, None, None], (shard_rows, head_ways, 1)),
            *terms_parts,
            jnp.zeros((shard_rows, head_ways, HEAD_WIDTH - 1 - 3 * query_heads), jnp.bfloat16),
        ],
        axis=2,
    )
    kvd_local = jnp.concatenate(
        [
            key_matrix.reshape(shard_rows, head_ways, kv_cols),
            value_matrix.reshape(shard_rows, head_ways, kv_cols),
            misc,
        ],
        axis=2,
    )
    kvd_local = lax.all_to_all(kvd_local, "head", split_axis=1, concat_axis=0, tiled=True)
    kvd_local = kvd_local.reshape(block_rows, 2 * kv_cols + HEAD_WIDTH)
    terms_at = 2 * kv_cols + 1
    row_terms_blk = (
        kvd_local[:, terms_at : terms_at + query_heads].astype(jnp.float32)
        + kvd_local[:, terms_at + query_heads : terms_at + 2 * query_heads].astype(jnp.float32)
    ) + kvd_local[:, terms_at + 2 * query_heads : terms_at + 3 * query_heads].astype(jnp.float32)
    packed = jnp.concatenate(
        [
            query_matrix.reshape(shard_rows, head_ways, q_cols),
            output_cotangent.reshape(shard_rows, head_ways, q_cols),
        ],
        axis=2,
    )
    packed = lax.all_to_all(packed, "head", split_axis=1, concat_axis=0, tiled=True)
    packed = packed.reshape(block_rows, 2 * q_cols)

    my_block = lax.axis_index("blk")
    query_segment = kvd_local[:, 2 * kv_cols].astype(jnp.float32)
    first_segment = query_segment[0]

    span = min(DOC_SPAN, cycle_size - 1)
    near_blocks = [kvd_local]
    for distance in range(1, span + 1):
        near_blocks.append(shifted(kvd_local, "blk", distance))
    flags = [jnp.int32(1)]
    for distance in range(1, span + 1):
        last_segment = near_blocks[distance][block_rows - 1, 2 * kv_cols].astype(jnp.float32)
        flags.append(((my_block - distance >= 0) & (last_segment == first_segment)).astype(jnp.int32))
    flags = jnp.stack(flags)
    near_keys = jnp.stack([kvd[:, :kv_cols] for kvd in near_blocks])
    near_values = jnp.stack([kvd[:, kv_cols : 2 * kv_cols] for kvd in near_blocks])
    near_docs = jnp.stack([kvd[:, 2 * kv_cols].astype(jnp.float32) for kvd in near_blocks])[:, :, None]
    query_total, key_parts, value_parts = block_attention(
        tile_flags(flags, query_segment, near_docs[:, :, 0]),
        packed[:, :q_cols],
        packed[:, q_cols : 2 * q_cols],
        row_terms_blk.transpose(1, 0)[:, None, :],
        query_segment[None, :],
        near_docs,
        near_keys,
        near_values,
    )
    my_group = lax.axis_index("head")
    query_grad = (query_total * logit_scale).astype(jnp.bfloat16)
    query_out = jnp.zeros((shard_rows, head_ways * q_cols), jnp.bfloat16)
    for step in range(head_ways):
        target = (my_group + step) % head_ways
        piece = lax.dynamic_slice_in_dim(query_grad, target * shard_rows, shard_rows, 0)
        if step > 0:
            piece = lax.ppermute(
                piece, "head", [(i, (i + step) % head_ways) for i in range(head_ways)]
            )
        source = (my_group - step) % head_ways
        query_out = lax.dynamic_update_slice_in_dim(query_out, piece, source * q_cols, 1)
    kv_grad = jnp.concatenate([key_parts[0], value_parts[0]], axis=1)
    for distance in range(1, span + 1):
        sent = jnp.concatenate([key_parts[distance], value_parts[distance]], axis=1)
        kv_grad = kv_grad + shifted(sent.astype(jnp.bfloat16), "blk", -distance).astype(
            jnp.float32
        )
    key_gradient = (kv_grad[:, :kv_cols] * logit_scale).astype(jnp.bfloat16)
    value_gradient = kv_grad[:, kv_cols:].astype(jnp.bfloat16)
    out_packed = jnp.concatenate([key_gradient, value_gradient], axis=1).reshape(
        head_ways, shard_rows, 1, 2 * kv_cols
    )
    out_packed = lax.all_to_all(out_packed, "head", split_axis=0, concat_axis=2, tiled=True)
    out_packed = out_packed.reshape(shard_rows, head_ways, 2 * kv_cols)
    return (
        query_out,
        out_packed[:, :, :kv_cols].reshape(shard_rows, head_ways * kv_cols),
        out_packed[:, :, kv_cols:].reshape(shard_rows, head_ways * kv_cols),
    )


def solution(mesh):
    return jax.shard_map(
        per_device,
        mesh=mesh,
        in_specs=(
            P(("blk", "head"), None),
            P(("blk", "head"), None),
            P(("blk", "head"), None),
            P(("blk", "head"), None),
            P(("blk", "head"), None),
            P(("blk", "head")),
        ),
        out_specs=(P(("blk", "head"), None), P(("blk", "head"), None), P(("blk", "head"), None)),
        check_vma=False,
    )
```

```python
import functools

import jax
import jax.numpy as jnp
from jax import lax
from jax.experimental import pallas as pl
from jax.experimental.pallas import tpu as pltpu
from jax.sharding import PartitionSpec as P

HEAD_WIDTH = 128
DOC_SPAN = 4


masked_score = -1e30


def shifted(block, axis, distance):
    devices = range(lax.axis_size(axis))
    route = [(i - distance, i) for i in devices if i - distance in devices]
    return lax.ppermute(block, axis, route)


def attn_kernel(flags_ref, q_ref, do_ref, rt_ref, qdoc_ref, kdoc_ref, k_ref, v_ref,
                dq_ref, dk_ref, dv_ref, bias_ref, scores_ref, m_ref, l_ref, *, n_near, logit_scale):
    head = pl.program_id(0)
    rows = q_ref.shape[0]

    @pl.when(head == 0)
    def _():
        dk_ref[...] = jnp.zeros_like(dk_ref)
        dv_ref[...] = jnp.zeros_like(dv_ref)
        key_id = lax.broadcasted_iota(jnp.int32, (rows, rows), 0)
        query_id = lax.broadcasted_iota(jnp.int32, (rows, rows), 1)
        qdoc = qdoc_ref[...]
        for d in range(n_near):
            @pl.when(flags_ref[d] > 0)
            def _():
                allowed = kdoc_ref[d] == qdoc
                if d == 0:
                    allowed = allowed & (key_id <= query_id)
                bias_ref[d] = jnp.where(allowed, 0.0, masked_score)

    q = q_ref[...]
    do = do_ref[...]

    def scores_of(d):
        s = lax.dot_general(k_ref[d], q, (((1,), (1,)), ((), ())),
                            preferred_element_type=jnp.float32)
        return s * logit_scale + bias_ref[d]

    m_ref[...] = jnp.full(m_ref.shape, masked_score, jnp.float32)
    l_ref[...] = jnp.zeros(l_ref.shape, jnp.float32)
    for d in range(n_near):
        @pl.when(flags_ref[d] > 0)
        def _():
            s = scores_of(d)
            scores_ref[d] = s
            m_old = m_ref[...]
            m_new = jnp.maximum(m_old, jnp.max(s, axis=0, keepdims=True))
            l_ref[...] = l_ref[...] * jnp.exp(m_old - m_new) + jnp.sum(
                jnp.exp(s - m_new), axis=0, keepdims=True)
            m_ref[...] = m_new

    log_total = m_ref[...] + jnp.log(l_ref[...])
    rt = rt_ref[0]
    dq_ref[...] = jnp.zeros_like(dq_ref)
    for d in range(n_near):
        @pl.when(flags_ref[d] > 0)
        def _():
            p = jnp.exp(scores_ref[d] - log_total)
            dp = lax.dot_general(v_ref[d], do, (((1,), (1,)), ((), ())),
                                 preferred_element_type=jnp.float32)
            ds = (p * (dp - rt)).astype(jnp.bfloat16)
            pb = p.astype(jnp.bfloat16)
            dv_ref[d] += jnp.dot(pb, do, preferred_element_type=jnp.float32)
            dk_ref[d] += jnp.dot(ds, q, preferred_element_type=jnp.float32)
            dq_ref[...] += lax.dot_general(ds, k_ref[d], (((0,), (0,)), ((), ())),
                                           preferred_element_type=jnp.float32)


def block_attention(flags, q, do, rt, qdoc, kdoc, k, v):
    rows, cols = q.shape
    heads = cols // HEAD_WIDTH
    n_near = k.shape[0]
    kern = functools.partial(attn_kernel, n_near=n_near, logit_scale=HEAD_WIDTH ** (-0.5))
    full3 = lambda shape: pl.BlockSpec(shape, lambda h, f: (0, 0, 0))
    flops = 2 * heads * n_near * rows * rows * HEAD_WIDTH * 6
    return pl.pallas_call(
        kern,
        out_shape=(
            jax.ShapeDtypeStruct((rows, cols), jnp.float32),
            jax.ShapeDtypeStruct((n_near, rows, HEAD_WIDTH), jnp.float32),
            jax.ShapeDtypeStruct((n_near, rows, HEAD_WIDTH), jnp.float32),
        ),
        grid_spec=pltpu.PrefetchScalarGridSpec(
            num_scalar_prefetch=1,
            grid=(heads,),
            in_specs=[
                pl.BlockSpec((rows, HEAD_WIDTH), lambda h, f: (0, h)),
                pl.BlockSpec((rows, HEAD_WIDTH), lambda h, f: (0, h)),
                pl.BlockSpec((1, 1, rows), lambda h, f: (h, 0, 0)),
                pl.BlockSpec((1, rows), lambda h, f: (0, 0)),
                full3((n_near, rows, 1)),
                full3((n_near, rows, HEAD_WIDTH)),
                full3((n_near, rows, HEAD_WIDTH)),
            ],
            out_specs=[
                pl.BlockSpec((rows, HEAD_WIDTH), lambda h, f: (0, h)),
                full3((n_near, rows, HEAD_WIDTH)),
                full3((n_near, rows, HEAD_WIDTH)),
            ],
            scratch_shapes=[
                pltpu.VMEM((n_near, rows, rows), jnp.float32),
                pltpu.VMEM((n_near, rows, rows), jnp.float32),
                pltpu.VMEM((1, rows), jnp.float32),
                pltpu.VMEM((1, rows), jnp.float32),
            ],
        ),
        compiler_params=pltpu.CompilerParams(dimension_semantics=("arbitrary",)),
        cost_estimate=pl.CostEstimate(flops=flops, transcendentals=2 * heads * n_near * rows * rows,
                                      bytes_accessed=4 * rows * cols * 2 + 8 * n_near * rows * HEAD_WIDTH * 2),
    )(flags, q, do, rt, qdoc, kdoc, k, v)


def per_device(query_matrix, key_matrix, value_matrix, output_cotangent, forward_output, doc_ids):
    cycle_size = lax.axis_size("blk")
    head_ways = lax.axis_size("head")
    shard_rows = query_matrix.shape[0]
    block_rows = shard_rows * head_ways
    query_heads = query_matrix.shape[1] // (HEAD_WIDTH * head_ways)
    kv_heads = key_matrix.shape[1] // (HEAD_WIDTH * head_ways)
    heads_per_group = query_heads // kv_heads
    q_cols = query_heads * HEAD_WIDTH
    kv_cols = kv_heads * HEAD_WIDTH
    logit_scale = HEAD_WIDTH ** (-0.5)
    all_heads = query_matrix.shape[1] // HEAD_WIDTH

    row_terms_local = jnp.sum(
        output_cotangent.astype(jnp.float32).reshape(shard_rows, all_heads, HEAD_WIDTH)
        * forward_output.astype(jnp.float32).reshape(shard_rows, all_heads, HEAD_WIDTH),
        axis=-1,
    ).reshape(shard_rows, head_ways, query_heads)
    terms_parts = []
    remainder = row_terms_local
    for _ in range(3):
        part = lax.reduce_precision(remainder, exponent_bits=8, mantissa_bits=7)
        terms_parts.append(part.astype(jnp.bfloat16))
        remainder = remainder - part
    misc = jnp.concatenate(
        [
            jnp.broadcast_to(doc_ids.astype(jnp.bfloat16)[:, None, None], (shard_rows, head_ways, 1)),
            *terms_parts,
            jnp.zeros((shard_rows, head_ways, HEAD_WIDTH - 1 - 3 * query_heads), jnp.bfloat16),
        ],
        axis=2,
    )
    kvd_local = jnp.concatenate(
        [
            key_matrix.reshape(shard_rows, head_ways, kv_cols),
            value_matrix.reshape(shard_rows, head_ways, kv_cols),
            misc,
        ],
        axis=2,
    )
    kvd_local = lax.all_to_all(kvd_local, "head", split_axis=1, concat_axis=0, tiled=True)
    kvd_local = kvd_local.reshape(block_rows, 2 * kv_cols + HEAD_WIDTH)
    terms_at = 2 * kv_cols + 1
    row_terms_blk = (
        kvd_local[:, terms_at : terms_at + query_heads].astype(jnp.float32)
        + kvd_local[:, terms_at + query_heads : terms_at + 2 * query_heads].astype(jnp.float32)
    ) + kvd_local[:, terms_at + 2 * query_heads : terms_at + 3 * query_heads].astype(jnp.float32)
    packed = jnp.concatenate(
        [
            query_matrix.reshape(shard_rows, head_ways, q_cols),
            output_cotangent.reshape(shard_rows, head_ways, q_cols),
        ],
        axis=2,
    )
    packed = lax.all_to_all(packed, "head", split_axis=1, concat_axis=0, tiled=True)
    packed = packed.reshape(block_rows, 2 * q_cols)

    my_block = lax.axis_index("blk")
    query_segment = kvd_local[:, 2 * kv_cols].astype(jnp.float32)
    first_segment = query_segment[0]

    span = min(DOC_SPAN, cycle_size - 1)
    near_blocks = [kvd_local]
    for distance in range(1, span + 1):
        near_blocks.append(shifted(kvd_local, "blk", distance))
    flags = [jnp.int32(1)]
    for distance in range(1, span + 1):
        last_segment = near_blocks[distance][block_rows - 1, 2 * kv_cols].astype(jnp.float32)
        flags.append(((my_block - distance >= 0) & (last_segment == first_segment)).astype(jnp.int32))
    flags = jnp.stack(flags)
    near_keys = jnp.stack([kvd[:, :kv_cols] for kvd in near_blocks])
    near_values = jnp.stack([kvd[:, kv_cols : 2 * kv_cols] for kvd in near_blocks])
    near_docs = jnp.stack([kvd[:, 2 * kv_cols].astype(jnp.float32) for kvd in near_blocks])[:, :, None]
    query_total, key_parts, value_parts = block_attention(
        flags,
        packed[:, :q_cols],
        packed[:, q_cols : 2 * q_cols],
        row_terms_blk.transpose(1, 0)[:, None, :],
        query_segment[None, :],
        near_docs,
        near_keys,
        near_values,
    )
    my_group = lax.axis_index("head")
    query_grad = (query_total * logit_scale).astype(jnp.bfloat16)
    query_out = jnp.zeros((shard_rows, head_ways * q_cols), jnp.bfloat16)
    for step in range(head_ways):
        target = (my_group + step) % head_ways
        piece = lax.dynamic_slice_in_dim(query_grad, target * shard_rows, shard_rows, 0)
        if step > 0:
            piece = lax.ppermute(
                piece, "head", [(i, (i + step) % head_ways) for i in range(head_ways)]
            )
        source = (my_group - step) % head_ways
        query_out = lax.dynamic_update_slice_in_dim(query_out, piece, source * q_cols, 1)
    kv_grad = jnp.concatenate([key_parts[0], value_parts[0]], axis=1)
    for distance in range(1, span + 1):
        sent = jnp.concatenate([key_parts[distance], value_parts[distance]], axis=1)
        kv_grad = kv_grad + shifted(sent.astype(jnp.bfloat16), "blk", -distance).astype(
            jnp.float32
        )
    key_gradient = (kv_grad[:, :kv_cols] * logit_scale).astype(jnp.bfloat16)
    value_gradient = kv_grad[:, kv_cols:].astype(jnp.bfloat16)
    out_packed = jnp.concatenate([key_gradient, value_gradient], axis=1).reshape(
        head_ways, shard_rows, 1, 2 * kv_cols
    )
    out_packed = lax.all_to_all(out_packed, "head", split_axis=0, concat_axis=2, tiled=True)
    out_packed = out_packed.reshape(shard_rows, head_ways, 2 * kv_cols)
    return (
        query_out,
        out_packed[:, :, :kv_cols].reshape(shard_rows, head_ways * kv_cols),
        out_packed[:, :, kv_cols:].reshape(shard_rows, head_ways * kv_cols),
    )


def solution(mesh):
    return jax.shard_map(
        per_device,
        mesh=mesh,
        in_specs=(
            P(("blk", "head"), None),
            P(("blk", "head"), None),
            P(("blk", "head"), None),
            P(("blk", "head"), None),
            P(("blk", "head"), None),
            P(("blk", "head")),
        ),
        out_specs=(P(("blk", "head"), None), P(("blk", "head"), None), P(("blk", "head"), None)),
        check_vma=False,
    )
```

```python
import functools

import jax
import jax.numpy as jnp
from jax import lax
from jax.experimental import pallas as pl
from jax.experimental.pallas import tpu as pltpu
from jax.sharding import PartitionSpec as P

HEAD_WIDTH = 128
DOC_SPAN = 4


masked_score = -1e30


def shifted(block, axis, distance):
    devices = range(lax.axis_size(axis))
    route = [(i - distance, i) for i in devices if i - distance in devices]
    return lax.ppermute(block, axis, route)


def attn_kernel(flags_ref, q_ref, do_ref, rt_ref, qdoc_ref, kdoc_ref, k_ref, v_ref,
                dq_ref, dk_ref, dv_ref, bias_ref, scores_ref, m_ref, l_ref, *, n_near, logit_scale):
    head = pl.program_id(0)
    rows = q_ref.shape[0]

    @pl.when(head == 0)
    def _():
        dk_ref[...] = jnp.zeros_like(dk_ref)
        dv_ref[...] = jnp.zeros_like(dv_ref)
        key_id = lax.broadcasted_iota(jnp.int32, (rows, rows), 0)
        query_id = lax.broadcasted_iota(jnp.int32, (rows, rows), 1)
        qdoc = qdoc_ref[...]
        for d in range(n_near):
            @pl.when(flags_ref[d] > 0)
            def _():
                allowed = kdoc_ref[d] == qdoc
                if d == 0:
                    allowed = allowed & (key_id <= query_id)
                bias_ref[d] = jnp.where(allowed, 0.0, masked_score)

    q = q_ref[...]
    do = do_ref[...]

    def scores_of(d):
        s = lax.dot_general(k_ref[d], q, (((1,), (1,)), ((), ())),
                            preferred_element_type=jnp.float32)
        return s * logit_scale + bias_ref[d]

    m_ref[...] = jnp.full(m_ref.shape, masked_score, jnp.float32)
    l_ref[...] = jnp.zeros(l_ref.shape, jnp.float32)
    for d in range(n_near):
        @pl.when(flags_ref[d] > 0)
        def _():
            s = scores_of(d)
            scores_ref[d] = s
            m_old = m_ref[...]
            m_new = jnp.maximum(m_old, jnp.max(s, axis=0, keepdims=True))
            l_ref[...] = l_ref[...] * jnp.exp(m_old - m_new) + jnp.sum(
                jnp.exp(s - m_new), axis=0, keepdims=True)
            m_ref[...] = m_new

    log_total = m_ref[...] + jnp.log(l_ref[...])
    rt = rt_ref[0]
    dq_ref[...] = jnp.zeros_like(dq_ref)
    for d in range(n_near):
        @pl.when(flags_ref[d] > 0)
        def _():
            p = jnp.exp(scores_ref[d] - log_total)
            dp = lax.dot_general(v_ref[d], do, (((1,), (1,)), ((), ())),
                                 preferred_element_type=jnp.float32)
            ds = (p * (dp - rt)).astype(jnp.bfloat16)
            pb = p.astype(jnp.bfloat16)
            dv_ref[d] += jnp.dot(pb, do, preferred_element_type=jnp.float32)
            dk_ref[d] += jnp.dot(ds, q, preferred_element_type=jnp.float32)
            dq_ref[...] += lax.dot_general(ds, k_ref[d], (((0,), (0,)), ((), ())),
                                           preferred_element_type=jnp.float32)


def block_attention(flags, q, do, rt, qdoc, kdoc, k, v):
    rows, cols = q.shape
    heads = cols // HEAD_WIDTH
    n_near = k.shape[0]
    kern = functools.partial(attn_kernel, n_near=n_near, logit_scale=HEAD_WIDTH ** (-0.5))
    full3 = lambda shape: pl.BlockSpec(shape, lambda h, f: (0, 0, 0))
    flops = 2 * heads * n_near * rows * rows * HEAD_WIDTH * 6
    return pl.pallas_call(
        kern,
        out_shape=(
            jax.ShapeDtypeStruct((rows, cols), jnp.float32),
            jax.ShapeDtypeStruct((n_near, rows, HEAD_WIDTH), jnp.float32),
            jax.ShapeDtypeStruct((n_near, rows, HEAD_WIDTH), jnp.float32),
        ),
        grid_spec=pltpu.PrefetchScalarGridSpec(
            num_scalar_prefetch=1,
            grid=(heads,),
            in_specs=[
                pl.BlockSpec((rows, HEAD_WIDTH), lambda h, f: (0, h)),
                pl.BlockSpec((rows, HEAD_WIDTH), lambda h, f: (0, h)),
                pl.BlockSpec((1, 1, rows), lambda h, f: (h, 0, 0)),
                pl.BlockSpec((1, rows), lambda h, f: (0, 0)),
                full3((n_near, rows, 1)),
                full3((n_near, rows, HEAD_WIDTH)),
                full3((n_near, rows, HEAD_WIDTH)),
            ],
            out_specs=[
                pl.BlockSpec((rows, HEAD_WIDTH), lambda h, f: (0, h)),
                full3((n_near, rows, HEAD_WIDTH)),
                full3((n_near, rows, HEAD_WIDTH)),
            ],
            scratch_shapes=[
                pltpu.VMEM((n_near, rows, rows), jnp.float32),
                pltpu.VMEM((n_near, rows, rows), jnp.float32),
                pltpu.VMEM((1, rows), jnp.float32),
                pltpu.VMEM((1, rows), jnp.float32),
            ],
        ),
        compiler_params=pltpu.CompilerParams(dimension_semantics=("arbitrary",)),
        cost_estimate=pl.CostEstimate(flops=flops, transcendentals=2 * heads * n_near * rows * rows,
                                      bytes_accessed=4 * rows * cols * 2 + 8 * n_near * rows * HEAD_WIDTH * 2),
    )(flags, q, do, rt, qdoc, kdoc, k, v)


def per_device(query_matrix, key_matrix, value_matrix, output_cotangent, forward_output, doc_ids):
    cycle_size = lax.axis_size("blk")
    head_ways = lax.axis_size("head")
    shard_rows = query_matrix.shape[0]
    block_rows = shard_rows * head_ways
    query_heads = query_matrix.shape[1] // (HEAD_WIDTH * head_ways)
    kv_heads = key_matrix.shape[1] // (HEAD_WIDTH * head_ways)
    heads_per_group = query_heads // kv_heads
    q_cols = query_heads * HEAD_WIDTH
    kv_cols = kv_heads * HEAD_WIDTH
    logit_scale = HEAD_WIDTH ** (-0.5)
    all_heads = query_matrix.shape[1] // HEAD_WIDTH

    row_terms_local = jnp.sum(
        output_cotangent.astype(jnp.float32).reshape(shard_rows, all_heads, HEAD_WIDTH)
        * forward_output.astype(jnp.float32).reshape(shard_rows, all_heads, HEAD_WIDTH),
        axis=-1,
    ).reshape(shard_rows, head_ways, query_heads)
    terms_parts = []
    remainder = row_terms_local
    for _ in range(3):
        part = lax.reduce_precision(remainder, exponent_bits=8, mantissa_bits=7)
        terms_parts.append(part.astype(jnp.bfloat16))
        remainder = remainder - part
    misc = jnp.concatenate(
        [
            jnp.broadcast_to(doc_ids.astype(jnp.bfloat16)[:, None, None], (shard_rows, head_ways, 1)),
            *terms_parts,
            jnp.zeros((shard_rows, head_ways, HEAD_WIDTH - 1 - 3 * query_heads), jnp.bfloat16),
        ],
        axis=2,
    )
    kvd_local = jnp.concatenate(
        [
            key_matrix.reshape(shard_rows, head_ways, kv_cols),
            value_matrix.reshape(shard_rows, head_ways, kv_cols),
            misc,
        ],
        axis=2,
    )
    kvd_local = lax.all_to_all(kvd_local, "head", split_axis=1, concat_axis=0, tiled=True)
    kvd_local = kvd_local.reshape(block_rows, 2 * kv_cols + HEAD_WIDTH)
    terms_at = 2 * kv_cols + 1
    row_terms_blk = (
        kvd_local[:, terms_at : terms_at + query_heads].astype(jnp.float32)
        + kvd_local[:, terms_at + query_heads : terms_at + 2 * query_heads].astype(jnp.float32)
    ) + kvd_local[:, terms_at + 2 * query_heads : terms_at + 3 * query_heads].astype(jnp.float32)
    half_heads = query_heads // 2
    half_cols = half_heads * HEAD_WIDTH
    query_split = query_matrix.reshape(shard_rows, head_ways, 2, half_cols)
    grad_split = output_cotangent.reshape(shard_rows, head_ways, 2, half_cols)
    first_half = jnp.concatenate([query_split[:, :, 0], grad_split[:, :, 0]], axis=2)
    second_half = jnp.concatenate([query_split[:, :, 1], grad_split[:, :, 1]], axis=2)
    first_half = lax.all_to_all(first_half, "head", split_axis=1, concat_axis=0, tiled=True)
    first_half, second_half = lax.optimization_barrier((first_half, second_half))
    second_half = lax.all_to_all(second_half, "head", split_axis=1, concat_axis=0, tiled=True)
    halves = [h.reshape(block_rows, 2 * half_cols) for h in (first_half, second_half)]

    my_block = lax.axis_index("blk")
    query_segment = kvd_local[:, 2 * kv_cols].astype(jnp.float32)
    first_segment = query_segment[0]

    span = min(DOC_SPAN, cycle_size - 1)
    near_blocks = [kvd_local]
    for distance in range(1, span + 1):
        near_blocks.append(shifted(kvd_local, "blk", distance))
    flags = [jnp.int32(1)]
    for distance in range(1, span + 1):
        last_segment = near_blocks[distance][block_rows - 1, 2 * kv_cols].astype(jnp.float32)
        flags.append(((my_block - distance >= 0) & (last_segment == first_segment)).astype(jnp.int32))
    flags = jnp.stack(flags)
    near_keys = jnp.stack([kvd[:, :kv_cols] for kvd in near_blocks])
    near_values = jnp.stack([kvd[:, kv_cols : 2 * kv_cols] for kvd in near_blocks])
    near_docs = jnp.stack([kvd[:, 2 * kv_cols].astype(jnp.float32) for kvd in near_blocks])[:, :, None]
    my_group = lax.axis_index("head")
    terms_rows = row_terms_blk.transpose(1, 0)[:, None, :]
    query_out = jnp.zeros((shard_rows, head_ways * q_cols), jnp.bfloat16)
    key_parts = value_parts = None
    for half in range(2):
        query_total, key_half, value_half = block_attention(
            flags,
            halves[half][:, :half_cols],
            halves[half][:, half_cols:],
            terms_rows[half * half_heads : (half + 1) * half_heads],
            query_segment[None, :],
            near_docs,
            near_keys,
            near_values,
        )
        query_grad = (query_total * logit_scale).astype(jnp.bfloat16)
        for step in range(head_ways):
            target = (my_group + step) % head_ways
            piece = lax.dynamic_slice_in_dim(query_grad, target * shard_rows, shard_rows, 0)
            if step > 0:
                piece = lax.ppermute(
                    piece, "head", [(i, (i + step) % head_ways) for i in range(head_ways)]
                )
            source = (my_group - step) % head_ways
            query_out = lax.dynamic_update_slice_in_dim(
                query_out, piece, source * q_cols + half * half_cols, 1
            )
        if key_parts is None:
            key_parts, value_parts = key_half, value_half
        else:
            key_parts, value_parts = key_parts + key_half, value_parts + value_half
    kv_grad = jnp.concatenate([key_parts[0], value_parts[0]], axis=1)
    for distance in range(1, span + 1):
        sent = jnp.concatenate([key_parts[distance], value_parts[distance]], axis=1)
        kv_grad = kv_grad + shifted(sent.astype(jnp.bfloat16), "blk", -distance).astype(
            jnp.float32
        )
    key_gradient = (kv_grad[:, :kv_cols] * logit_scale).astype(jnp.bfloat16)
    value_gradient = kv_grad[:, kv_cols:].astype(jnp.bfloat16)
    out_packed = jnp.concatenate([key_gradient, value_gradient], axis=1).reshape(
        head_ways, shard_rows, 1, 2 * kv_cols
    )
    out_packed = lax.all_to_all(out_packed, "head", split_axis=0, concat_axis=2, tiled=True)
    out_packed = out_packed.reshape(shard_rows, head_ways, 2 * kv_cols)
    return (
        query_out,
        out_packed[:, :, :kv_cols].reshape(shard_rows, head_ways * kv_cols),
        out_packed[:, :, kv_cols:].reshape(shard_rows, head_ways * kv_cols),
    )


def solution(mesh):
    return jax.shard_map(
        per_device,
        mesh=mesh,
        in_specs=(
            P(("blk", "head"), None),
            P(("blk", "head"), None),
            P(("blk", "head"), None),
            P(("blk", "head"), None),
            P(("blk", "head"), None),
            P(("blk", "head")),
        ),
        out_specs=(P(("blk", "head"), None), P(("blk", "head"), None), P(("blk", "head"), None)),
        check_vma=False,
    )
```

```python
import functools

import jax
import jax.numpy as jnp
from jax import lax
from jax.experimental import pallas as pl
from jax.experimental.pallas import tpu as pltpu
from jax.sharding import PartitionSpec as P

HEAD_WIDTH = 128
DOC_SPAN = 4


masked_score = -1e30


def shifted(block, axis, distance):
    devices = range(lax.axis_size(axis))
    route = [(i - distance, i) for i in devices if i - distance in devices]
    return lax.ppermute(block, axis, route)


def attn_kernel(flags_ref, q_ref, do_ref, rt_ref, qdoc_ref, kdoc_ref, k_ref, v_ref,
                dq_ref, dk_ref, dv_ref, bias_ref, scores_ref, m_ref, l_ref, *, n_near, logit_scale):
    head = pl.program_id(0)
    rows = q_ref.shape[0]

    @pl.when(head == 0)
    def _():
        dk_ref[...] = jnp.zeros_like(dk_ref)
        dv_ref[...] = jnp.zeros_like(dv_ref)
        key_id = lax.broadcasted_iota(jnp.int32, (rows, rows), 0)
        query_id = lax.broadcasted_iota(jnp.int32, (rows, rows), 1)
        qdoc = qdoc_ref[...]
        for d in range(n_near):
            @pl.when(flags_ref[d] > 0)
            def _():
                allowed = kdoc_ref[d] == qdoc
                if d == 0:
                    allowed = allowed & (key_id <= query_id)
                bias_ref[d] = jnp.where(allowed, 0.0, masked_score)

    q = q_ref[...]
    do = do_ref[...]

    def scores_of(d):
        s = lax.dot_general(k_ref[d], q, (((1,), (1,)), ((), ())),
                            preferred_element_type=jnp.float32)
        return s * logit_scale + bias_ref[d]

    m_ref[...] = jnp.full(m_ref.shape, masked_score, jnp.float32)
    l_ref[...] = jnp.zeros(l_ref.shape, jnp.float32)
    for d in range(n_near):
        @pl.when(flags_ref[d] > 0)
        def _():
            s = scores_of(d)
            scores_ref[d] = s
            m_old = m_ref[...]
            m_new = jnp.maximum(m_old, jnp.max(s, axis=0, keepdims=True))
            l_ref[...] = l_ref[...] * jnp.exp(m_old - m_new) + jnp.sum(
                jnp.exp(s - m_new), axis=0, keepdims=True)
            m_ref[...] = m_new

    log_total = m_ref[...] + jnp.log(l_ref[...])
    rt = rt_ref[0]
    dq_ref[...] = jnp.zeros_like(dq_ref)
    for d in range(n_near):
        @pl.when(flags_ref[d] > 0)
        def _():
            p = jnp.exp(scores_ref[d] - log_total)
            dp = lax.dot_general(v_ref[d], do, (((1,), (1,)), ((), ())),
                                 preferred_element_type=jnp.float32)
            ds = (p * (dp - rt)).astype(jnp.bfloat16)
            pb = p.astype(jnp.bfloat16)
            dv_ref[d] += jnp.dot(pb, do, preferred_element_type=jnp.float32)
            dk_ref[d] += jnp.dot(ds, q, preferred_element_type=jnp.float32)
            dq_ref[...] += lax.dot_general(ds, k_ref[d], (((0,), (0,)), ((), ())),
                                           preferred_element_type=jnp.float32)


def block_attention(flags, q, do, rt, qdoc, kdoc, k, v):
    rows, cols = q.shape
    heads = cols // HEAD_WIDTH
    n_near = k.shape[0]
    kern = functools.partial(attn_kernel, n_near=n_near, logit_scale=HEAD_WIDTH ** (-0.5))
    full3 = lambda shape: pl.BlockSpec(shape, lambda h, f: (0, 0, 0))
    flops = 2 * heads * n_near * rows * rows * HEAD_WIDTH * 6
    return pl.pallas_call(
        kern,
        out_shape=(
            jax.ShapeDtypeStruct((rows, cols), jnp.float32),
            jax.ShapeDtypeStruct((n_near, rows, HEAD_WIDTH), jnp.float32),
            jax.ShapeDtypeStruct((n_near, rows, HEAD_WIDTH), jnp.float32),
        ),
        grid_spec=pltpu.PrefetchScalarGridSpec(
            num_scalar_prefetch=1,
            grid=(heads,),
            in_specs=[
                pl.BlockSpec((rows, HEAD_WIDTH), lambda h, f: (0, h)),
                pl.BlockSpec((rows, HEAD_WIDTH), lambda h, f: (0, h)),
                pl.BlockSpec((1, 1, rows), lambda h, f: (h, 0, 0)),
                pl.BlockSpec((1, rows), lambda h, f: (0, 0)),
                full3((n_near, rows, 1)),
                full3((n_near, rows, HEAD_WIDTH)),
                full3((n_near, rows, HEAD_WIDTH)),
            ],
            out_specs=[
                pl.BlockSpec((rows, HEAD_WIDTH), lambda h, f: (0, h)),
                full3((n_near, rows, HEAD_WIDTH)),
                full3((n_near, rows, HEAD_WIDTH)),
            ],
            scratch_shapes=[
                pltpu.VMEM((n_near, rows, rows), jnp.float32),
                pltpu.VMEM((n_near, rows, rows), jnp.float32),
                pltpu.VMEM((1, rows), jnp.float32),
                pltpu.VMEM((1, rows), jnp.float32),
            ],
        ),
        compiler_params=pltpu.CompilerParams(dimension_semantics=("arbitrary",)),
        cost_estimate=pl.CostEstimate(flops=flops, transcendentals=2 * heads * n_near * rows * rows,
                                      bytes_accessed=4 * rows * cols * 2 + 8 * n_near * rows * HEAD_WIDTH * 2),
    )(flags, q, do, rt, qdoc, kdoc, k, v)


def per_device(query_matrix, key_matrix, value_matrix, output_cotangent, forward_output, doc_ids):
    cycle_size = lax.axis_size("blk")
    head_ways = lax.axis_size("head")
    shard_rows = query_matrix.shape[0]
    block_rows = shard_rows * head_ways
    query_heads = query_matrix.shape[1] // (HEAD_WIDTH * head_ways)
    kv_heads = key_matrix.shape[1] // (HEAD_WIDTH * head_ways)
    heads_per_group = query_heads // kv_heads
    q_cols = query_heads * HEAD_WIDTH
    kv_cols = kv_heads * HEAD_WIDTH
    logit_scale = HEAD_WIDTH ** (-0.5)
    all_heads = query_matrix.shape[1] // HEAD_WIDTH

    row_terms_local = jnp.sum(
        output_cotangent.astype(jnp.float32).reshape(shard_rows, all_heads, HEAD_WIDTH)
        * forward_output.astype(jnp.float32).reshape(shard_rows, all_heads, HEAD_WIDTH),
        axis=-1,
    ).reshape(shard_rows, head_ways, query_heads)
    terms_parts = []
    remainder = row_terms_local
    for _ in range(3):
        part = lax.reduce_precision(remainder, exponent_bits=8, mantissa_bits=7)
        terms_parts.append(part.astype(jnp.bfloat16))
        remainder = remainder - part
    misc = jnp.concatenate(
        [
            jnp.broadcast_to(doc_ids.astype(jnp.bfloat16)[:, None, None], (shard_rows, head_ways, 1)),
            *terms_parts,
            jnp.zeros((shard_rows, head_ways, HEAD_WIDTH - 1 - 3 * query_heads), jnp.bfloat16),
        ],
        axis=2,
    )
    kvd_local = jnp.concatenate(
        [
            key_matrix.reshape(shard_rows, head_ways, kv_cols),
            value_matrix.reshape(shard_rows, head_ways, kv_cols),
            misc,
        ],
        axis=2,
    )
    kvd_shard = kvd_local
    half_heads = query_heads // 2
    half_cols = half_heads * HEAD_WIDTH
    query_split = query_matrix.reshape(shard_rows, head_ways, 2, half_cols)
    grad_split = output_cotangent.reshape(shard_rows, head_ways, 2, half_cols)
    first_half = jnp.concatenate([query_split[:, :, 0], grad_split[:, :, 0], kvd_shard], axis=2)
    second_half = jnp.concatenate([query_split[:, :, 1], grad_split[:, :, 1]], axis=2)
    first_half = lax.all_to_all(first_half, "head", split_axis=1, concat_axis=0, tiled=True)
    first_half, second_half = lax.optimization_barrier((first_half, second_half))
    second_half = lax.all_to_all(second_half, "head", split_axis=1, concat_axis=0, tiled=True)
    first_half = first_half.reshape(block_rows, 2 * half_cols + 2 * kv_cols + HEAD_WIDTH)
    kvd_local = first_half[:, 2 * half_cols :]
    halves = [first_half[:, : 2 * half_cols], second_half.reshape(block_rows, 2 * half_cols)]
    terms_at = 2 * kv_cols + 1
    row_terms_blk = (
        kvd_local[:, terms_at : terms_at + query_heads].astype(jnp.float32)
        + kvd_local[:, terms_at + query_heads : terms_at + 2 * query_heads].astype(jnp.float32)
    ) + kvd_local[:, terms_at + 2 * query_heads : terms_at + 3 * query_heads].astype(jnp.float32)

    my_block = lax.axis_index("blk")
    query_segment = kvd_local[:, 2 * kv_cols].astype(jnp.float32)
    first_segment = query_segment[0]

    span = min(DOC_SPAN, cycle_size - 1)
    near_blocks = [kvd_local]
    for distance in range(1, span + 1):
        near_blocks.append(shifted(kvd_local, "blk", distance))
    flags = [jnp.int32(1)]
    for distance in range(1, span + 1):
        last_segment = near_blocks[distance][block_rows - 1, 2 * kv_cols].astype(jnp.float32)
        flags.append(((my_block - distance >= 0) & (last_segment == first_segment)).astype(jnp.int32))
    flags = jnp.stack(flags)
    near_keys = jnp.stack([kvd[:, :kv_cols] for kvd in near_blocks])
    near_values = jnp.stack([kvd[:, kv_cols : 2 * kv_cols] for kvd in near_blocks])
    near_docs = jnp.stack([kvd[:, 2 * kv_cols].astype(jnp.float32) for kvd in near_blocks])[:, :, None]
    my_group = lax.axis_index("head")
    terms_rows = row_terms_blk.transpose(1, 0)[:, None, :]
    query_out = jnp.zeros((shard_rows, head_ways * q_cols), jnp.bfloat16)
    key_parts = value_parts = None
    for half in range(2):
        query_total, key_half, value_half = block_attention(
            flags,
            halves[half][:, :half_cols],
            halves[half][:, half_cols:],
            terms_rows[half * half_heads : (half + 1) * half_heads],
            query_segment[None, :],
            near_docs,
            near_keys,
            near_values,
        )
        query_grad = (query_total * logit_scale).astype(jnp.bfloat16)
        for step in range(head_ways):
            target = (my_group + step) % head_ways
            piece = lax.dynamic_slice_in_dim(query_grad, target * shard_rows, shard_rows, 0)
            if step > 0:
                piece = lax.ppermute(
                    piece, "head", [(i, (i + step) % head_ways) for i in range(head_ways)]
                )
            source = (my_group - step) % head_ways
            query_out = lax.dynamic_update_slice_in_dim(
                query_out, piece, source * q_cols + half * half_cols, 1
            )
        if key_parts is None:
            key_parts, value_parts = key_half, value_half
        else:
            key_parts, value_parts = key_parts + key_half, value_parts + value_half
    kv_grad = jnp.concatenate([key_parts[0], value_parts[0]], axis=1)
    for distance in range(1, span + 1):
        sent = jnp.concatenate([key_parts[distance], value_parts[distance]], axis=1)
        kv_grad = kv_grad + shifted(sent.astype(jnp.bfloat16), "blk", -distance).astype(
            jnp.float32
        )
    key_gradient = (kv_grad[:, :kv_cols] * logit_scale).astype(jnp.bfloat16)
    value_gradient = kv_grad[:, kv_cols:].astype(jnp.bfloat16)
    out_packed = jnp.concatenate([key_gradient, value_gradient], axis=1).reshape(
        head_ways, shard_rows, 1, 2 * kv_cols
    )
    out_packed = lax.all_to_all(out_packed, "head", split_axis=0, concat_axis=2, tiled=True)
    out_packed = out_packed.reshape(shard_rows, head_ways, 2 * kv_cols)
    return (
        query_out,
        out_packed[:, :, :kv_cols].reshape(shard_rows, head_ways * kv_cols),
        out_packed[:, :, kv_cols:].reshape(shard_rows, head_ways * kv_cols),
    )


def solution(mesh):
    return jax.shard_map(
        per_device,
        mesh=mesh,
        in_specs=(
            P(("blk", "head"), None),
            P(("blk", "head"), None),
            P(("blk", "head"), None),
            P(("blk", "head"), None),
            P(("blk", "head"), None),
            P(("blk", "head")),
        ),
        out_specs=(P(("blk", "head"), None), P(("blk", "head"), None), P(("blk", "head"), None)),
        check_vma=False,
    )
```

```python
import functools

import jax
import jax.numpy as jnp
from jax import lax
from jax.experimental import pallas as pl
from jax.experimental.pallas import tpu as pltpu
from jax.sharding import PartitionSpec as P

HEAD_WIDTH = 128
DOC_SPAN = 4


masked_score = -1e30


def shifted(block, axis, distance):
    devices = range(lax.axis_size(axis))
    route = [(i - distance, i) for i in devices if i - distance in devices]
    return lax.ppermute(block, axis, route)


def attn_kernel(flags_ref, q_ref, do_ref, rt_ref, qdoc_ref, kdoc_ref, k_ref, v_ref,
                dq_ref, dk_ref, dv_ref, bias_ref, scores_ref, m_ref, l_ref, *, n_near, logit_scale):
    head = pl.program_id(0)
    rows = q_ref.shape[0]

    @pl.when(head == 0)
    def _():
        dk_ref[...] = jnp.zeros_like(dk_ref)
        dv_ref[...] = jnp.zeros_like(dv_ref)
        key_id = lax.broadcasted_iota(jnp.int32, (rows, rows), 0)
        query_id = lax.broadcasted_iota(jnp.int32, (rows, rows), 1)
        qdoc = qdoc_ref[...]
        for d in range(n_near):
            @pl.when(flags_ref[d] > 0)
            def _():
                allowed = kdoc_ref[d] == qdoc
                if d == 0:
                    allowed = allowed & (key_id <= query_id)
                bias_ref[d] = jnp.where(allowed, 0.0, masked_score)

    q = q_ref[...]
    do = do_ref[...]

    def scores_of(d):
        s = lax.dot_general(k_ref[d], q, (((1,), (1,)), ((), ())),
                            preferred_element_type=jnp.float32)
        return s * logit_scale + bias_ref[d]

    half = rows // 2
    low, high = pl.ds(0, half), pl.ds(half, half)
    upper = lax.dot_general(k_ref[0, low, :], q, (((1,), (1,)), ((), ())),
                            preferred_element_type=jnp.float32) * logit_scale + bias_ref[0, low, :]
    lower = lax.dot_general(k_ref[0, high, :], q_ref[high, :], (((1,), (1,)), ((), ())),
                            preferred_element_type=jnp.float32) * logit_scale + bias_ref[0, high, high]
    scores_ref[0, low, :] = upper
    scores_ref[0, high, high] = lower
    m_first = jnp.max(upper, axis=0, keepdims=True)
    m_last = jnp.maximum(m_first[:, half:], jnp.max(lower, axis=0, keepdims=True))
    m_ref[:, low] = m_first[:, :half]
    m_ref[:, high] = m_last
    l_first = jnp.sum(jnp.exp(upper - m_ref[...]), axis=0, keepdims=True)
    l_ref[:, low] = l_first[:, :half]
    l_ref[:, high] = l_first[:, half:] + jnp.sum(jnp.exp(lower - m_last), axis=0, keepdims=True)
    for d in range(1, n_near):
        @pl.when(flags_ref[d] > 0)
        def _():
            s = scores_of(d)
            scores_ref[d] = s
            m_old = m_ref[...]
            m_new = jnp.maximum(m_old, jnp.max(s, axis=0, keepdims=True))
            l_ref[...] = l_ref[...] * jnp.exp(m_old - m_new) + jnp.sum(
                jnp.exp(s - m_new), axis=0, keepdims=True)
            m_ref[...] = m_new

    log_total = m_ref[...] + jnp.log(l_ref[...])
    rt = rt_ref[0]
    p = jnp.exp(scores_ref[0, low, :] - log_total)
    dp = lax.dot_general(v_ref[0, low, :], do, (((1,), (1,)), ((), ())),
                         preferred_element_type=jnp.float32)
    ds = (p * (dp - rt)).astype(jnp.bfloat16)
    dv_ref[0, low, :] += jnp.dot(p.astype(jnp.bfloat16), do, preferred_element_type=jnp.float32)
    dk_ref[0, low, :] += jnp.dot(ds, q, preferred_element_type=jnp.float32)
    dq_ref[...] = lax.dot_general(ds, k_ref[0, low, :], (((0,), (0,)), ((), ())),
                                  preferred_element_type=jnp.float32)
    p = jnp.exp(scores_ref[0, high, high] - log_total[:, half:])
    dp = lax.dot_general(v_ref[0, high, :], do_ref[high, :], (((1,), (1,)), ((), ())),
                         preferred_element_type=jnp.float32)
    ds = (p * (dp - rt[:, half:])).astype(jnp.bfloat16)
    dv_ref[0, high, :] += jnp.dot(p.astype(jnp.bfloat16), do_ref[high, :],
                                  preferred_element_type=jnp.float32)
    dk_ref[0, high, :] += jnp.dot(ds, q_ref[high, :], preferred_element_type=jnp.float32)
    dq_ref[high, :] += lax.dot_general(ds, k_ref[0, high, :], (((0,), (0,)), ((), ())),
                                       preferred_element_type=jnp.float32)
    for d in range(1, n_near):
        @pl.when(flags_ref[d] > 0)
        def _():
            p = jnp.exp(scores_ref[d] - log_total)
            dp = lax.dot_general(v_ref[d], do, (((1,), (1,)), ((), ())),
                                 preferred_element_type=jnp.float32)
            ds = (p * (dp - rt)).astype(jnp.bfloat16)
            pb = p.astype(jnp.bfloat16)
            dv_ref[d] += jnp.dot(pb, do, preferred_element_type=jnp.float32)
            dk_ref[d] += jnp.dot(ds, q, preferred_element_type=jnp.float32)
            dq_ref[...] += lax.dot_general(ds, k_ref[d], (((0,), (0,)), ((), ())),
                                           preferred_element_type=jnp.float32)


def block_attention(flags, q, do, rt, qdoc, kdoc, k, v):
    rows, cols = q.shape
    heads = cols // HEAD_WIDTH
    n_near = k.shape[0]
    kern = functools.partial(attn_kernel, n_near=n_near, logit_scale=HEAD_WIDTH ** (-0.5))
    full3 = lambda shape: pl.BlockSpec(shape, lambda h, f: (0, 0, 0))
    flops = 2 * heads * n_near * rows * rows * HEAD_WIDTH * 6
    return pl.pallas_call(
        kern,
        out_shape=(
            jax.ShapeDtypeStruct((rows, cols), jnp.float32),
            jax.ShapeDtypeStruct((n_near, rows, HEAD_WIDTH), jnp.float32),
            jax.ShapeDtypeStruct((n_near, rows, HEAD_WIDTH), jnp.float32),
        ),
        grid_spec=pltpu.PrefetchScalarGridSpec(
            num_scalar_prefetch=1,
            grid=(heads,),
            in_specs=[
                pl.BlockSpec((rows, HEAD_WIDTH), lambda h, f: (0, h)),
                pl.BlockSpec((rows, HEAD_WIDTH), lambda h, f: (0, h)),
                pl.BlockSpec((1, 1, rows), lambda h, f: (h, 0, 0)),
                pl.BlockSpec((1, rows), lambda h, f: (0, 0)),
                full3((n_near, rows, 1)),
                full3((n_near, rows, HEAD_WIDTH)),
                full3((n_near, rows, HEAD_WIDTH)),
            ],
            out_specs=[
                pl.BlockSpec((rows, HEAD_WIDTH), lambda h, f: (0, h)),
                full3((n_near, rows, HEAD_WIDTH)),
                full3((n_near, rows, HEAD_WIDTH)),
            ],
            scratch_shapes=[
                pltpu.VMEM((n_near, rows, rows), jnp.float32),
                pltpu.VMEM((n_near, rows, rows), jnp.float32),
                pltpu.VMEM((1, rows), jnp.float32),
                pltpu.VMEM((1, rows), jnp.float32),
            ],
        ),
        compiler_params=pltpu.CompilerParams(dimension_semantics=("arbitrary",)),
        cost_estimate=pl.CostEstimate(flops=flops, transcendentals=2 * heads * n_near * rows * rows,
                                      bytes_accessed=4 * rows * cols * 2 + 8 * n_near * rows * HEAD_WIDTH * 2),
    )(flags, q, do, rt, qdoc, kdoc, k, v)


def per_device(query_matrix, key_matrix, value_matrix, output_cotangent, forward_output, doc_ids):
    cycle_size = lax.axis_size("blk")
    head_ways = lax.axis_size("head")
    shard_rows = query_matrix.shape[0]
    block_rows = shard_rows * head_ways
    query_heads = query_matrix.shape[1] // (HEAD_WIDTH * head_ways)
    kv_heads = key_matrix.shape[1] // (HEAD_WIDTH * head_ways)
    heads_per_group = query_heads // kv_heads
    q_cols = query_heads * HEAD_WIDTH
    kv_cols = kv_heads * HEAD_WIDTH
    logit_scale = HEAD_WIDTH ** (-0.5)
    all_heads = query_matrix.shape[1] // HEAD_WIDTH

    row_terms_local = jnp.sum(
        output_cotangent.astype(jnp.float32).reshape(shard_rows, all_heads, HEAD_WIDTH)
        * forward_output.astype(jnp.float32).reshape(shard_rows, all_heads, HEAD_WIDTH),
        axis=-1,
    ).reshape(shard_rows, head_ways, query_heads)
    terms_parts = []
    remainder = row_terms_local
    for _ in range(3):
        part = lax.reduce_precision(remainder, exponent_bits=8, mantissa_bits=7)
        terms_parts.append(part.astype(jnp.bfloat16))
        remainder = remainder - part
    misc = jnp.concatenate(
        [
            jnp.broadcast_to(doc_ids.astype(jnp.bfloat16)[:, None, None], (shard_rows, head_ways, 1)),
            *terms_parts,
            jnp.zeros((shard_rows, head_ways, HEAD_WIDTH - 1 - 3 * query_heads), jnp.bfloat16),
        ],
        axis=2,
    )
    kvd_local = jnp.concatenate(
        [
            key_matrix.reshape(shard_rows, head_ways, kv_cols),
            value_matrix.reshape(shard_rows, head_ways, kv_cols),
            misc,
        ],
        axis=2,
    )
    kvd_local = lax.all_to_all(kvd_local, "head", split_axis=1, concat_axis=0, tiled=True)
    kvd_local = kvd_local.reshape(block_rows, 2 * kv_cols + HEAD_WIDTH)
    terms_at = 2 * kv_cols + 1
    row_terms_blk = (
        kvd_local[:, terms_at : terms_at + query_heads].astype(jnp.float32)
        + kvd_local[:, terms_at + query_heads : terms_at + 2 * query_heads].astype(jnp.float32)
    ) + kvd_local[:, terms_at + 2 * query_heads : terms_at + 3 * query_heads].astype(jnp.float32)
    packed = jnp.concatenate(
        [
            query_matrix.reshape(shard_rows, head_ways, q_cols),
            output_cotangent.reshape(shard_rows, head_ways, q_cols),
        ],
        axis=2,
    )
    packed = lax.all_to_all(packed, "head", split_axis=1, concat_axis=0, tiled=True)
    packed = packed.reshape(block_rows, 2 * q_cols)

    my_block = lax.axis_index("blk")
    query_segment = kvd_local[:, 2 * kv_cols].astype(jnp.float32)
    first_segment = query_segment[0]

    span = min(DOC_SPAN, cycle_size - 1)
    near_blocks = [kvd_local]
    for distance in range(1, span + 1):
        near_blocks.append(shifted(kvd_local, "blk", distance))
    flags = [jnp.int32(1)]
    for distance in range(1, span + 1):
        last_segment = near_blocks[distance][block_rows - 1, 2 * kv_cols].astype(jnp.float32)
        flags.append(((my_block - distance >= 0) & (last_segment == first_segment)).astype(jnp.int32))
    flags = jnp.stack(flags)
    near_keys = jnp.stack([kvd[:, :kv_cols] for kvd in near_blocks])
    near_values = jnp.stack([kvd[:, kv_cols : 2 * kv_cols] for kvd in near_blocks])
    near_docs = jnp.stack([kvd[:, 2 * kv_cols].astype(jnp.float32) for kvd in near_blocks])[:, :, None]
    query_total, key_parts, value_parts = block_attention(
        flags,
        packed[:, :q_cols],
        packed[:, q_cols : 2 * q_cols],
        row_terms_blk.transpose(1, 0)[:, None, :],
        query_segment[None, :],
        near_docs,
        near_keys,
        near_values,
    )
    my_group = lax.axis_index("head")
    query_grad = (query_total * logit_scale).astype(jnp.bfloat16)
    query_out = jnp.zeros((shard_rows, head_ways * q_cols), jnp.bfloat16)
    for step in range(head_ways):
        target = (my_group + step) % head_ways
        piece = lax.dynamic_slice_in_dim(query_grad, target * shard_rows, shard_rows, 0)
        if step > 0:
            piece = lax.ppermute(
                piece, "head", [(i, (i + step) % head_ways) for i in range(head_ways)]
            )
        source = (my_group - step) % head_ways
        query_out = lax.dynamic_update_slice_in_dim(query_out, piece, source * q_cols, 1)
    kv_grad = jnp.concatenate([key_parts[0], value_parts[0]], axis=1)
    for distance in range(1, span + 1):
        sent = jnp.concatenate([key_parts[distance], value_parts[distance]], axis=1)
        kv_grad = kv_grad + shifted(sent.astype(jnp.bfloat16), "blk", -distance).astype(
            jnp.float32
        )
    key_gradient = (kv_grad[:, :kv_cols] * logit_scale).astype(jnp.bfloat16)
    value_gradient = kv_grad[:, kv_cols:].astype(jnp.bfloat16)
    out_packed = jnp.concatenate([key_gradient, value_gradient], axis=1).reshape(
        head_ways, shard_rows, 1, 2 * kv_cols
    )
    out_packed = lax.all_to_all(out_packed, "head", split_axis=0, concat_axis=2, tiled=True)
    out_packed = out_packed.reshape(shard_rows, head_ways, 2 * kv_cols)
    return (
        query_out,
        out_packed[:, :, :kv_cols].reshape(shard_rows, head_ways * kv_cols),
        out_packed[:, :, kv_cols:].reshape(shard_rows, head_ways * kv_cols),
    )


def solution(mesh):
    return jax.shard_map(
        per_device,
        mesh=mesh,
        in_specs=(
            P(("blk", "head"), None),
            P(("blk", "head"), None),
            P(("blk", "head"), None),
            P(("blk", "head"), None),
            P(("blk", "head"), None),
            P(("blk", "head")),
        ),
        out_specs=(P(("blk", "head"), None), P(("blk", "head"), None), P(("blk", "head"), None)),
        check_vma=False,
    )
```

```python
import functools

import jax
import jax.numpy as jnp
from jax import lax
from jax.experimental import pallas as pl
from jax.experimental.pallas import tpu as pltpu
from jax.sharding import PartitionSpec as P

HEAD_WIDTH = 128
DOC_SPAN = 4


masked_score = -1e30


def shifted(block, axis, distance):
    devices = range(lax.axis_size(axis))
    route = [(i - distance, i) for i in devices if i - distance in devices]
    return lax.ppermute(block, axis, route)


def attn_kernel(flags_ref, q_ref, do_ref, rt_ref, qdoc_ref, kdoc_ref, k_ref, v_ref,
                dq_ref, dk_ref, dv_ref, bias_ref, scores_ref, m_ref, l_ref, *, n_near, logit_scale):
    head = pl.program_id(0)
    rows = q_ref.shape[0]

    @pl.when(head == 0)
    def _():
        dk_ref[...] = jnp.zeros_like(dk_ref)
        dv_ref[...] = jnp.zeros_like(dv_ref)
        key_id = lax.broadcasted_iota(jnp.int32, (rows, rows), 0)
        query_id = lax.broadcasted_iota(jnp.int32, (rows, rows), 1)
        qdoc = qdoc_ref[...]
        for d in range(n_near):
            @pl.when(flags_ref[d] == 1)
            def _():
                allowed = kdoc_ref[d] == qdoc
                if d == 0:
                    allowed = allowed & (key_id <= query_id)
                bias_ref[d] = jnp.where(allowed, 0.0, masked_score)

    q = q_ref[...]
    do = do_ref[...]

    def scores_of(d):
        s = lax.dot_general(k_ref[d], q, (((1,), (1,)), ((), ())),
                            preferred_element_type=jnp.float32)
        return s * logit_scale + bias_ref[d]

    half = rows // 2
    low, high = pl.ds(0, half), pl.ds(half, half)
    upper = lax.dot_general(k_ref[0, low, :], q, (((1,), (1,)), ((), ())),
                            preferred_element_type=jnp.float32) * logit_scale + bias_ref[0, low, :]
    lower = lax.dot_general(k_ref[0, high, :], q_ref[high, :], (((1,), (1,)), ((), ())),
                            preferred_element_type=jnp.float32) * logit_scale + bias_ref[0, high, high]
    scores_ref[0, low, :] = upper
    scores_ref[0, high, high] = lower
    m_first = jnp.max(upper, axis=0, keepdims=True)
    m_last = jnp.maximum(m_first[:, half:], jnp.max(lower, axis=0, keepdims=True))
    m_ref[:, low] = m_first[:, :half]
    m_ref[:, high] = m_last
    l_first = jnp.sum(jnp.exp(upper - m_ref[...]), axis=0, keepdims=True)
    l_ref[:, low] = l_first[:, :half]
    l_ref[:, high] = l_first[:, half:] + jnp.sum(jnp.exp(lower - m_last), axis=0, keepdims=True)
    for d in range(1, n_near):
        @pl.when(flags_ref[d] > 0)
        def _():
            s = lax.dot_general(k_ref[d], q, (((1,), (1,)), ((), ())),
                                preferred_element_type=jnp.float32) * logit_scale
            s = lax.cond(flags_ref[d] == 1, lambda t: t + bias_ref[d], lambda t: t, s)
            scores_ref[d] = s
            m_old = m_ref[...]
            m_new = jnp.maximum(m_old, jnp.max(s, axis=0, keepdims=True))
            l_ref[...] = l_ref[...] * jnp.exp(m_old - m_new) + jnp.sum(
                jnp.exp(s - m_new), axis=0, keepdims=True)
            m_ref[...] = m_new

    log_total = m_ref[...] + jnp.log(l_ref[...])
    rt = rt_ref[0]
    p = jnp.exp(scores_ref[0, low, :] - log_total)
    dp = lax.dot_general(v_ref[0, low, :], do, (((1,), (1,)), ((), ())),
                         preferred_element_type=jnp.float32)
    ds = (p * (dp - rt)).astype(jnp.bfloat16)
    dv_ref[0, low, :] += jnp.dot(p.astype(jnp.bfloat16), do, preferred_element_type=jnp.float32)
    dk_ref[0, low, :] += jnp.dot(ds, q, preferred_element_type=jnp.float32)
    dq_ref[...] = lax.dot_general(ds, k_ref[0, low, :], (((0,), (0,)), ((), ())),
                                  preferred_element_type=jnp.float32)
    p = jnp.exp(scores_ref[0, high, high] - log_total[:, half:])
    dp = lax.dot_general(v_ref[0, high, :], do_ref[high, :], (((1,), (1,)), ((), ())),
                         preferred_element_type=jnp.float32)
    ds = (p * (dp - rt[:, half:])).astype(jnp.bfloat16)
    dv_ref[0, high, :] += jnp.dot(p.astype(jnp.bfloat16), do_ref[high, :],
                                  preferred_element_type=jnp.float32)
    dk_ref[0, high, :] += jnp.dot(ds, q_ref[high, :], preferred_element_type=jnp.float32)
    dq_ref[high, :] += lax.dot_general(ds, k_ref[0, high, :], (((0,), (0,)), ((), ())),
                                       preferred_element_type=jnp.float32)
    for d in range(1, n_near):
        @pl.when(flags_ref[d] > 0)
        def _():
            p = jnp.exp(scores_ref[d] - log_total)
            dp = lax.dot_general(v_ref[d], do, (((1,), (1,)), ((), ())),
                                 preferred_element_type=jnp.float32)
            ds = (p * (dp - rt)).astype(jnp.bfloat16)
            pb = p.astype(jnp.bfloat16)
            dv_ref[d] += jnp.dot(pb, do, preferred_element_type=jnp.float32)
            dk_ref[d] += jnp.dot(ds, q, preferred_element_type=jnp.float32)
            dq_ref[...] += lax.dot_general(ds, k_ref[d], (((0,), (0,)), ((), ())),
                                           preferred_element_type=jnp.float32)


def block_attention(flags, q, do, rt, qdoc, kdoc, k, v):
    rows, cols = q.shape
    heads = cols // HEAD_WIDTH
    n_near = k.shape[0]
    kern = functools.partial(attn_kernel, n_near=n_near, logit_scale=HEAD_WIDTH ** (-0.5))
    full3 = lambda shape: pl.BlockSpec(shape, lambda h, f: (0, 0, 0))
    flops = 2 * heads * n_near * rows * rows * HEAD_WIDTH * 6
    return pl.pallas_call(
        kern,
        out_shape=(
            jax.ShapeDtypeStruct((rows, cols), jnp.float32),
            jax.ShapeDtypeStruct((n_near, rows, HEAD_WIDTH), jnp.float32),
            jax.ShapeDtypeStruct((n_near, rows, HEAD_WIDTH), jnp.float32),
        ),
        grid_spec=pltpu.PrefetchScalarGridSpec(
            num_scalar_prefetch=1,
            grid=(heads,),
            in_specs=[
                pl.BlockSpec((rows, HEAD_WIDTH), lambda h, f: (0, h)),
                pl.BlockSpec((rows, HEAD_WIDTH), lambda h, f: (0, h)),
                pl.BlockSpec((1, 1, rows), lambda h, f: (h, 0, 0)),
                pl.BlockSpec((1, rows), lambda h, f: (0, 0)),
                full3((n_near, rows, 1)),
                full3((n_near, rows, HEAD_WIDTH)),
                full3((n_near, rows, HEAD_WIDTH)),
            ],
            out_specs=[
                pl.BlockSpec((rows, HEAD_WIDTH), lambda h, f: (0, h)),
                full3((n_near, rows, HEAD_WIDTH)),
                full3((n_near, rows, HEAD_WIDTH)),
            ],
            scratch_shapes=[
                pltpu.VMEM((n_near, rows, rows), jnp.float32),
                pltpu.VMEM((n_near, rows, rows), jnp.float32),
                pltpu.VMEM((1, rows), jnp.float32),
                pltpu.VMEM((1, rows), jnp.float32),
            ],
        ),
        compiler_params=pltpu.CompilerParams(dimension_semantics=("arbitrary",)),
        cost_estimate=pl.CostEstimate(flops=flops, transcendentals=2 * heads * n_near * rows * rows,
                                      bytes_accessed=4 * rows * cols * 2 + 8 * n_near * rows * HEAD_WIDTH * 2),
    )(flags, q, do, rt, qdoc, kdoc, k, v)


def per_device(query_matrix, key_matrix, value_matrix, output_cotangent, forward_output, doc_ids):
    cycle_size = lax.axis_size("blk")
    head_ways = lax.axis_size("head")
    shard_rows = query_matrix.shape[0]
    block_rows = shard_rows * head_ways
    query_heads = query_matrix.shape[1] // (HEAD_WIDTH * head_ways)
    kv_heads = key_matrix.shape[1] // (HEAD_WIDTH * head_ways)
    heads_per_group = query_heads // kv_heads
    q_cols = query_heads * HEAD_WIDTH
    kv_cols = kv_heads * HEAD_WIDTH
    logit_scale = HEAD_WIDTH ** (-0.5)
    all_heads = query_matrix.shape[1] // HEAD_WIDTH

    row_terms_local = jnp.sum(
        output_cotangent.astype(jnp.float32).reshape(shard_rows, all_heads, HEAD_WIDTH)
        * forward_output.astype(jnp.float32).reshape(shard_rows, all_heads, HEAD_WIDTH),
        axis=-1,
    ).reshape(shard_rows, head_ways, query_heads)
    terms_parts = []
    remainder = row_terms_local
    for _ in range(3):
        part = lax.reduce_precision(remainder, exponent_bits=8, mantissa_bits=7)
        terms_parts.append(part.astype(jnp.bfloat16))
        remainder = remainder - part
    misc = jnp.concatenate(
        [
            jnp.broadcast_to(doc_ids.astype(jnp.bfloat16)[:, None, None], (shard_rows, head_ways, 1)),
            *terms_parts,
            jnp.zeros((shard_rows, head_ways, HEAD_WIDTH - 1 - 3 * query_heads), jnp.bfloat16),
        ],
        axis=2,
    )
    kvd_local = jnp.concatenate(
        [
            key_matrix.reshape(shard_rows, head_ways, kv_cols),
            value_matrix.reshape(shard_rows, head_ways, kv_cols),
            misc,
        ],
        axis=2,
    )
    kvd_local = lax.all_to_all(kvd_local, "head", split_axis=1, concat_axis=0, tiled=True)
    kvd_local = kvd_local.reshape(block_rows, 2 * kv_cols + HEAD_WIDTH)
    terms_at = 2 * kv_cols + 1
    row_terms_blk = (
        kvd_local[:, terms_at : terms_at + query_heads].astype(jnp.float32)
        + kvd_local[:, terms_at + query_heads : terms_at + 2 * query_heads].astype(jnp.float32)
    ) + kvd_local[:, terms_at + 2 * query_heads : terms_at + 3 * query_heads].astype(jnp.float32)
    packed = jnp.concatenate(
        [
            query_matrix.reshape(shard_rows, head_ways, q_cols),
            output_cotangent.reshape(shard_rows, head_ways, q_cols),
        ],
        axis=2,
    )
    packed = lax.all_to_all(packed, "head", split_axis=1, concat_axis=0, tiled=True)
    packed = packed.reshape(block_rows, 2 * q_cols)

    my_block = lax.axis_index("blk")
    query_segment = kvd_local[:, 2 * kv_cols].astype(jnp.float32)
    first_segment = query_segment[0]

    span = min(DOC_SPAN, cycle_size - 1)
    near_blocks = [kvd_local]
    for distance in range(1, span + 1):
        near_blocks.append(shifted(kvd_local, "blk", distance))
    flags = [jnp.int32(1)]
    for distance in range(1, span + 1):
        last_segment = near_blocks[distance][block_rows - 1, 2 * kv_cols].astype(jnp.float32)
        shared = (my_block - distance >= 0) & (last_segment == first_segment)
        whole = near_blocks[distance][0, 2 * kv_cols].astype(jnp.float32) == query_segment[-1]
        flags.append(shared.astype(jnp.int32) * (1 + whole.astype(jnp.int32)))
    flags = jnp.stack(flags)
    near_keys = jnp.stack([kvd[:, :kv_cols] for kvd in near_blocks])
    near_values = jnp.stack([kvd[:, kv_cols : 2 * kv_cols] for kvd in near_blocks])
    near_docs = jnp.stack([kvd[:, 2 * kv_cols].astype(jnp.float32) for kvd in near_blocks])[:, :, None]
    query_total, key_parts, value_parts = block_attention(
        flags,
        packed[:, :q_cols],
        packed[:, q_cols : 2 * q_cols],
        row_terms_blk.transpose(1, 0)[:, None, :],
        query_segment[None, :],
        near_docs,
        near_keys,
        near_values,
    )
    my_group = lax.axis_index("head")
    query_grad = (query_total * logit_scale).astype(jnp.bfloat16)
    query_out = jnp.zeros((shard_rows, head_ways * q_cols), jnp.bfloat16)
    for step in range(head_ways):
        target = (my_group + step) % head_ways
        piece = lax.dynamic_slice_in_dim(query_grad, target * shard_rows, shard_rows, 0)
        if step > 0:
            piece = lax.ppermute(
                piece, "head", [(i, (i + step) % head_ways) for i in range(head_ways)]
            )
        source = (my_group - step) % head_ways
        query_out = lax.dynamic_update_slice_in_dim(query_out, piece, source * q_cols, 1)
    kv_grad = jnp.concatenate([key_parts[0], value_parts[0]], axis=1)
    for distance in range(1, span + 1):
        sent = jnp.concatenate([key_parts[distance], value_parts[distance]], axis=1)
        kv_grad = kv_grad + shifted(sent.astype(jnp.bfloat16), "blk", -distance).astype(
            jnp.float32
        )
    key_gradient = (kv_grad[:, :kv_cols] * logit_scale).astype(jnp.bfloat16)
    value_gradient = kv_grad[:, kv_cols:].astype(jnp.bfloat16)
    out_packed = jnp.concatenate([key_gradient, value_gradient], axis=1).reshape(
        head_ways, shard_rows, 1, 2 * kv_cols
    )
    out_packed = lax.all_to_all(out_packed, "head", split_axis=0, concat_axis=2, tiled=True)
    out_packed = out_packed.reshape(shard_rows, head_ways, 2 * kv_cols)
    return (
        query_out,
        out_packed[:, :, :kv_cols].reshape(shard_rows, head_ways * kv_cols),
        out_packed[:, :, kv_cols:].reshape(shard_rows, head_ways * kv_cols),
    )


def solution(mesh):
    return jax.shard_map(
        per_device,
        mesh=mesh,
        in_specs=(
            P(("blk", "head"), None),
            P(("blk", "head"), None),
            P(("blk", "head"), None),
            P(("blk", "head"), None),
            P(("blk", "head"), None),
            P(("blk", "head")),
        ),
        out_specs=(P(("blk", "head"), None), P(("blk", "head"), None), P(("blk", "head"), None)),
        check_vma=False,
    )
```
